32 devices in a mesh: ctx: 16 (over z, x, core), fsdp: 2 (over y).
Axes of the slice: x: 2, y: 2, z: 4, core: 2. Of those that a mesh axis runs over, the one named last changes fastest.
Arguments:
- activations: bfloat16 [4096, 8192], P('ctx', 'fsdp'), may hold values from -8.5 to 8.5
- w_query: bfloat16 [8192, 8192], P('ctx', 'fsdp'), may hold values from -0.044194174 to 0.044194174
- w_key: bfloat16 [8192, 1024], P('ctx', 'fsdp'), may hold values from -0.044194174 to 0.044194174
- w_value: bfloat16 [8192, 1024], P('ctx', 'fsdp'), may hold values from -0.0625 to 0.0625
- seed_words: int32 [1], replicated, may hold values from 0 to 1073741823
- stream_offset: int32 [1], replicated, may hold values from 0 to 1048575
- layer_index: int32 [1], replicated, may hold values from 0 to 79
Outputs:
- attention: bfloat16 [4096, 8192], P('ctx', 'fsdp')
The draws below stay inside these ranges and needn't reach their ends.
All inputs are finite; a program needn't handle non-finite values.
Results may differ from the reference program's by a relative error of at most 0.007.
Values may be sent and summed in bfloat16 or wider, within the bound.
No kernel may reach another device: no remote copies, remote signals or barrier semaphores. Data moves between devices by JAX's collectives and lax.ppermute only.
A program may use at most 320 MiB of HBM per device.

```python
import math
import jax
import jax.numpy as jnp
from jax import lax

D = 8192
HQ = 64
KV = 8
HD = 128
TOKENS = 4096


def weight_pair(key):
    spread = D ** (-0.5)
    query_part = jax.random.normal(jax.random.fold_in(key, 102), (D, KV, HQ // KV, HD), jnp.float32)
    key_part = jax.random.normal(jax.random.fold_in(key, 103), (D, KV, HD), jnp.float32)
    bound_value = 4.0 * spread
    query_weight = jnp.clip(query_part.reshape(D, HQ * HD) * spread, -bound_value, bound_value)
    key_weight = jnp.clip(key_part.reshape(D, KV * HD) * spread, -bound_value, bound_value)
    return (query_weight, key_weight)


def draw_w_query(key, part):
    return weight_pair(key)[0].astype(jnp.bfloat16)


def draw_w_key(key, part):
    return weight_pair(key)[1].astype(jnp.bfloat16)


def draw_activations(key, part):
    entries = jax.random.normal(jax.random.fold_in(key, 1), (TOKENS, D), jnp.float32)
    return jnp.clip(entries, -8.5, 8.5).astype(jnp.bfloat16)


def level_of(rng, shape, shards, low, high):
    def one(dim, shards_of):
        steps = jax.random.uniform(jax.random.fold_in(jax.random.fold_in(rng, 6), dim), (shards_of,), jnp.float32, low / len(shards), high / len(shards))
        return jnp.repeat(jnp.exp(steps), shape[dim] // shards_of).reshape((-1,) + (1,) * (len(shape) - dim - 1))

    gain = one(*shards[0])
    for cut in shards[1:]:
        gain = gain * one(*cut)
    return gain


def scatter_about(rng, extent, scale, limit, split=(), kind=jnp.bfloat16):
    result = scale * jax.random.normal(rng, extent, jnp.float32)
    if split:
        result = result * level_of(rng, extent, split, -0.22, 0.18)
    return jnp.clip(result, -limit, limit).astype(kind)


def setup_inputs(seed: int = 0) -> dict:
    streams_of = jax.random.split(jax.random.key(seed), 8)
    activations = draw_activations(jax.random.fold_in(streams_of[7], 71), 0)
    w_query = draw_w_query(jax.random.fold_in(streams_of[7], 71), 0)
    w_key = draw_w_key(jax.random.fold_in(streams_of[7], 71), 0)
    w_value = scatter_about(streams_of[3], (D, KV * HD), D ** -0.5, 0.0625, ((0, 16), (1, 2)))
    seed_words = jax.random.randint(streams_of[4], (1,), 0, 1073741824).astype(jnp.int32)
    stream_offset = jax.random.randint(streams_of[5], (1,), 0, 1048576).astype(jnp.int32)
    layer_index = jax.random.randint(streams_of[6], (1,), 0, 80).astype(jnp.int32)
    return dict(activations=activations, w_query=w_query, w_key=w_key, w_value=w_value, seed_words=seed_words, stream_offset=stream_offset, layer_index=layer_index)


golden = -1640531535
drop_rate = 0.1
drop_level = 1677722
rope_theta = 500000.0
masked_score = -1.0e30


def shift_down(values, amount):
    return lax.shift_right_logical(values, jnp.full(values.shape, amount, jnp.int32))


def scramble(values):
    values = jnp.bitwise_xor(values, shift_down(values, 16))
    values = values * jnp.int32(-2048144789)
    values = jnp.bitwise_xor(values, shift_down(values, 13))
    values = values * jnp.int32(-1028477387)
    return jnp.bitwise_xor(values, shift_down(values, 16))


def head_word(seed_words, stream_offset, layer_index, head_ids):
    inner = scramble(head_ids + stream_offset[0])
    middle = scramble(layer_index[0] * jnp.int32(golden) + inner)
    return scramble(seed_words[0] + middle)


def keep_factor(row_words, key_positions):
    mixed_bits = scramble(row_words[:, None] + key_positions[None, :] * jnp.int32(golden))
    return shift_down(mixed_bits, 8) >= drop_level


def rotate(values, positions):
    half_width = values.shape[-1] // 2
    exponent = jnp.arange(half_width, dtype=jnp.float32) * 2.0 / values.shape[-1]
    frequency = rope_theta ** (-exponent)
    angles = positions.astype(jnp.float32)[:, None] * frequency[None, :]
    cosine = jnp.cos(angles)
    sine_part = jnp.sin(angles)
    first_half = values[..., :half_width]
    second_half = values[..., half_width:]
    return jnp.concatenate([first_half * cosine - second_half * sine_part, second_half * cosine + first_half * sine_part], axis=-1)


def project(activations, weight, heads):
    mixed = jnp.dot(activations, weight, preferred_element_type=jnp.float32)
    return mixed.reshape(activations.shape[0], heads, HD).transpose(1, 0, 2)


def reference(activations, w_query, w_key, w_value, seed_words, stream_offset, layer_index):
    length = activations.shape[0]
    positions = jnp.arange(length, dtype=jnp.int32)
    queries = rotate(project(activations, w_query, HQ), positions).astype(jnp.bfloat16)
    keys = rotate(project(activations, w_key, KV), positions).astype(jnp.bfloat16)
    values = project(activations, w_value, KV).astype(jnp.bfloat16)
    query_block = math.gcd(length, 1024)

    def one_head(head_id):
        group = head_id // (HQ // KV)
        key_rows = keys[group].astype(jnp.float32)
        value_rows = values[group]
        head_queries = queries[head_id]
        word = head_word(seed_words, stream_offset, layer_index, head_id)

        def one_block(block_id):
            first_row = block_id * query_block
            query_rows = lax.dynamic_slice_in_dim(head_queries, first_row, query_block, 0).astype(jnp.float32)
            query_pos = first_row + jnp.arange(query_block, dtype=jnp.int32)
            scores = jnp.dot(query_rows, key_rows.T, preferred_element_type=jnp.float32, precision=lax.Precision.HIGHEST) * (HD ** -0.5)
            visible = positions[None, :] <= query_pos[:, None]
            highest = jnp.max(jnp.where(visible, scores, masked_score), axis=1, keepdims=True)
            weights = jnp.where(visible, jnp.exp(scores - highest), 0.0)
            summed = jnp.sum(weights, axis=1)
            keep = keep_factor(scramble(jnp.bitwise_xor(word, query_pos)), positions)
            dropped = jnp.where(keep, weights, 0.0).astype(jnp.bfloat16)
            mixed = jnp.dot(dropped, value_rows, preferred_element_type=jnp.float32)
            return (mixed / (summed * (1.0 - drop_rate))[:, None]).astype(jnp.bfloat16)

        blocks = lax.map(one_block, jnp.arange(length // query_block, dtype=jnp.int32))
        return blocks.reshape(length, HD)

    heads = lax.map(one_head, jnp.arange(HQ, dtype=jnp.int32))
    return heads.transpose(1, 0, 2).reshape(length, HQ * HD)
```

```python
import jax
import jax.numpy as jnp
import numpy as np
from jax import lax
from jax.sharding import Mesh
from jax.sharding import PartitionSpec as P

HQ = 64
KV = 8
HD = 128


golden = -1640531535
drop_rate = 0.1
drop_level = 1677722
rope_theta = 500000.0
masked_score = -1e30


def shift_down(values, amount):
    return lax.shift_right_logical(values, jnp.full(values.shape, amount, jnp.int32))


def scramble(values):
    values = jnp.bitwise_xor(values, shift_down(values, 16))
    values = values * jnp.int32(-2048144789)
    values = jnp.bitwise_xor(values, shift_down(values, 13))
    values = values * jnp.int32(-1028477387)
    return jnp.bitwise_xor(values, shift_down(values, 16))


def head_word(seed_words, stream_offset, layer_index, head_ids):
    inner = scramble(head_ids + stream_offset[0])
    middle = scramble(layer_index[0] * jnp.int32(golden) + inner)
    return scramble(seed_words[0] + middle)


def rotation(positions):
    half_width = HD // 2
    exponent = jnp.arange(half_width, dtype=jnp.float32) * 2.0 / HD
    frequency = rope_theta ** (-exponent)
    angles = positions.astype(jnp.float32)[:, None] * frequency[None, :]
    return jnp.cos(angles), jnp.sin(angles)


def rotate(values, cosine, sine_part):
    half_width = HD // 2
    first_half = values[..., :half_width]
    second_half = values[..., half_width:]
    return jnp.concatenate(
        [
            first_half * cosine - second_half * sine_part,
            second_half * cosine + first_half * sine_part,
        ],
        axis=-1,
    )


def shards(activations, w_query, w_key, w_value, seed_words, stream_offset, layer_index):
    n_g = lax.axis_size("cg")
    n_t = lax.axis_size("ct")
    g = lax.axis_index("cg")
    t = lax.axis_index("ct")
    f = lax.axis_index("fsdp")
    tok = activations.shape[0]
    d_rows = w_query.shape[0]
    group_heads = HQ // KV
    local_heads = w_query.shape[1] // HD
    qcols = group_heads * HD
    rows = n_g * tok

    full_rows = lax.all_gather(activations, "fsdp", axis=1, tiled=True)
    grp_rows = lax.all_gather(full_rows, "cg", axis=0, tiled=True)

    local_w = jnp.concatenate(
        [
            w_query.reshape(d_rows, n_g, qcols),
            w_key.reshape(d_rows, n_g, HD),
            w_value.reshape(d_rows, n_g, HD),
        ],
        axis=2,
    )
    mine = lax.all_to_all(local_w, "cg", split_axis=1, concat_axis=0, tiled=True)
    mine = mine.reshape(n_g, d_rows, qcols + 2 * HD)
    every = lax.all_gather(mine, "ct", axis=0, tiled=False)
    every = every.transpose(1, 0, 2, 3).reshape(n_g * n_t * d_rows, qcols + 2 * HD)

    mixed = jnp.dot(grp_rows, every, preferred_element_type=jnp.float32)
    chunk_of_row = n_t * (jnp.arange(rows, dtype=jnp.int32) // tok) + t
    positions = chunk_of_row * tok + jnp.arange(rows, dtype=jnp.int32) % tok
    cosine, sine_part = rotation(positions)
    queries = rotate(
        mixed[:, :qcols].reshape(rows, group_heads, HD), cosine[:, None, :], sine_part[:, None, :]
    ).astype(jnp.bfloat16)
    keys = rotate(mixed[:, qcols : qcols + HD], cosine, sine_part).astype(jnp.bfloat16)
    values = mixed[:, qcols + HD :].astype(jnp.bfloat16)

    pair = jnp.stack([keys, values], axis=1)
    pair = lax.all_gather(pair, "ct", axis=0, tiled=False)
    pair = pair.reshape(n_t, n_g, tok, 2, HD).transpose(1, 0, 2, 3, 4)
    pair = pair.reshape(n_g * n_t * tok, 2, HD)
    all_keys = pair[:, 0]
    all_values = pair[:, 1]

    head_global = f * local_heads + g * group_heads + jnp.arange(group_heads, dtype=jnp.int32)
    words = head_word(seed_words, stream_offset, layer_index, head_global)
    score_scale = HD ** (-0.5)
    pieces = []
    for chunk in range(n_g):
        span = n_t * (chunk + 1) * tok
        query_pos = (n_t * chunk + t) * tok + jnp.arange(tok, dtype=jnp.int32)
        key_pos = jnp.arange(span, dtype=jnp.int32)
        chunk_queries = queries[chunk * tok : (chunk + 1) * tok]
        scores = (
            jnp.einsum(
                "qhe,ke->hqk",
                chunk_queries,
                all_keys[:span],
                preferred_element_type=jnp.float32,
            )
            * score_scale
        )
        visible = key_pos[None, None, :] <= query_pos[None, :, None]
        highest = jnp.max(jnp.where(visible, scores, masked_score), axis=2, keepdims=True)
        weights = jnp.where(visible, jnp.exp(scores - highest), 0.0)
        summed = jnp.sum(weights, axis=2)
        row_words = scramble(jnp.bitwise_xor(words[:, None], query_pos[None, :]))
        mixed_bits = scramble(row_words[:, :, None] + (key_pos * jnp.int32(golden))[None, None, :])
        keep = shift_down(mixed_bits, 8) >= drop_level
        dropped = jnp.where(keep, weights, 0.0).astype(jnp.bfloat16)
        attended = jnp.einsum(
            "hqk,ke->hqe", dropped, all_values[:span], preferred_element_type=jnp.float32
        )
        result = (attended / (summed * (1.0 - drop_rate))[:, :, None]).astype(jnp.bfloat16)
        pieces.append(result.transpose(1, 0, 2).reshape(tok, qcols))
    out_rows = jnp.stack(pieces, axis=0)
    returned = lax.all_to_all(out_rows, "cg", split_axis=0, concat_axis=2, tiled=True)
    return returned.reshape(tok, n_g * qcols)


def solution(mesh):
    ctx = mesh.shape["ctx"]
    fsdp = mesh.shape["fsdp"]
    n_g = KV // fsdp
    n_t = ctx // n_g
    order = [mesh.axis_names.index("ctx"), mesh.axis_names.index("fsdp")]
    devices = np.transpose(mesh.devices, order).reshape(n_g, n_t, fsdp)
    grid = Mesh(devices, ("cg", "ct", "fsdp"))
    spec = P(("cg", "ct"), "fsdp")
    placed = (spec, spec, spec, spec, P(), P(), P())
    return jax.shard_map(shards, mesh=grid, in_specs=placed, out_specs=spec, check_vma=False)
```

```python
import jax
import jax.numpy as jnp
import numpy as np
from jax import lax
from jax.sharding import Mesh
from jax.sharding import PartitionSpec as P

HQ = 64
KV = 8
HD = 128


golden = -1640531535
drop_rate = 0.1
drop_level = 1677722
rope_theta = 500000.0
masked_score = -1e30


def shift_down(values, amount):
    return lax.shift_right_logical(values, jnp.full(values.shape, amount, jnp.int32))


def scramble(values):
    values = jnp.bitwise_xor(values, shift_down(values, 16))
    values = values * jnp.int32(-2048144789)
    values = jnp.bitwise_xor(values, shift_down(values, 13))
    values = values * jnp.int32(-1028477387)
    return jnp.bitwise_xor(values, shift_down(values, 16))


def head_word(seed_words, stream_offset, layer_index, head_ids):
    inner = scramble(head_ids + stream_offset[0])
    middle = scramble(layer_index[0] * jnp.int32(golden) + inner)
    return scramble(seed_words[0] + middle)


def rotation(positions):
    half_width = HD // 2
    exponent = jnp.arange(half_width, dtype=jnp.float32) * 2.0 / HD
    frequency = rope_theta ** (-exponent)
    angles = positions.astype(jnp.float32)[:, None] * frequency[None, :]
    return jnp.cos(angles), jnp.sin(angles)


def rotate(values, cosine, sine_part):
    half_width = HD // 2
    first_half = values[..., :half_width]
    second_half = values[..., half_width:]
    return jnp.concatenate(
        [
            first_half * cosine - second_half * sine_part,
            second_half * cosine + first_half * sine_part,
        ],
        axis=-1,
    )


def attend(queries, keys, values, query_pos, words, spans):
    score_scale = HD ** (-0.5)
    pieces = []
    for first, count, span in spans:
        block_pos = query_pos[first : first + count]
        key_pos = jnp.arange(span, dtype=jnp.int32)
        scores = (
            jnp.einsum(
                "qhe,ke->hqk",
                queries[first : first + count],
                keys[:span],
                preferred_element_type=jnp.float32,
            )
            * score_scale
        )
        visible = key_pos[None, None, :] <= block_pos[None, :, None]
        highest = jnp.max(jnp.where(visible, scores, masked_score), axis=2, keepdims=True)
        weights = jnp.where(visible, jnp.exp(scores - highest), 0.0)
        summed = jnp.sum(weights, axis=2)
        row_words = scramble(jnp.bitwise_xor(words[:, None], block_pos[None, :]))
        mixed_bits = scramble(row_words[:, :, None] + (key_pos * jnp.int32(golden))[None, None, :])
        keep = shift_down(mixed_bits, 8) >= drop_level
        dropped = jnp.where(keep, weights, 0.0).astype(jnp.bfloat16)
        attended = jnp.einsum(
            "hqk,ke->qhe", dropped, values[:span], preferred_element_type=jnp.float32
        )
        pieces.append(
            (attended / (summed * (1.0 - drop_rate)).T[:, :, None]).astype(jnp.bfloat16)
        )
    return jnp.concatenate(pieces, axis=0)


def shards(activations, w_query, w_key, w_value, seed_words, stream_offset, layer_index):
    n_t = lax.axis_size("ct")
    n_g = lax.axis_size("cg")
    t = lax.axis_index("ct")
    g = lax.axis_index("cg")
    f = lax.axis_index("fsdp")
    tok = activations.shape[0]
    d_rows = w_query.shape[0]
    group_heads = HQ // KV
    local_heads = w_query.shape[1] // HD
    qcols = group_heads * HD
    width = qcols + 2 * HD
    rows = n_g * tok
    length = n_t * rows

    half_rows = lax.all_gather(activations, "cg", axis=0, tiled=True)
    grp_rows = lax.all_gather(half_rows, "fsdp", axis=1, tiled=True)

    local_w = jnp.concatenate(
        [
            w_query.reshape(d_rows, n_g, qcols),
            w_key.reshape(d_rows, n_g, HD),
            w_value.reshape(d_rows, n_g, HD),
        ],
        axis=2,
    )
    received = [lax.dynamic_index_in_dim(local_w, g, 1, keepdims=False)]
    for shift in range(1, n_g):
        outgoing = lax.dynamic_index_in_dim(local_w, (g + shift) % n_g, 1, keepdims=False)
        perm = [(i, (i + shift) % n_g) for i in range(n_g)]
        received.append(lax.ppermute(outgoing, "cg", perm))
    by_shift = jnp.stack(received, axis=0)
    mine = jnp.take(by_shift, (g - jnp.arange(n_g, dtype=jnp.int32)) % n_g, axis=0)
    every = lax.all_gather(mine, "ct", axis=0, tiled=False).reshape(n_t * n_g * d_rows, width)

    mixed = jnp.dot(grp_rows, every, preferred_element_type=jnp.float32)
    positions = t * rows + jnp.arange(rows, dtype=jnp.int32)
    cosine, sine_part = rotation(positions)
    queries = rotate(
        mixed[:, :qcols].reshape(rows, group_heads, HD), cosine[:, None, :], sine_part[:, None, :]
    ).astype(jnp.bfloat16)
    keys = rotate(mixed[:, qcols : qcols + HD], cosine, sine_part).astype(jnp.bfloat16)
    values = mixed[:, qcols + HD :].astype(jnp.bfloat16)

    pair = lax.all_gather(jnp.stack([keys, values], axis=1), "ct", axis=0, tiled=True)
    all_keys = pair[:, 0]
    all_values = pair[:, 1]

    if group_heads % n_t == 0:
        owned = group_heads // n_t
        spread = lax.all_to_all(
            queries.reshape(rows, n_t, owned, HD), "ct", split_axis=1, concat_axis=0, tiled=True
        ).reshape(length, owned, HD)
        head_local = g * group_heads + t * owned + jnp.arange(owned, dtype=jnp.int32)
        words = head_word(seed_words, stream_offset, layer_index, f * local_heads + head_local)
        block = min(length, 512)
        spans = [(i * block, block, (i + 1) * block) for i in range(length // block)]
        out = attend(
            spread, all_keys, all_values, jnp.arange(length, dtype=jnp.int32), words, spans
        )
        out = lax.all_to_all(
            out.reshape(n_t, rows, owned, HD), "ct", split_axis=0, concat_axis=2, tiled=True
        ).reshape(rows, qcols)
    else:
        head_local = g * group_heads + jnp.arange(group_heads, dtype=jnp.int32)
        words = head_word(seed_words, stream_offset, layer_index, f * local_heads + head_local)
        out = attend(queries, all_keys, all_values, positions, words, [(0, rows, length)])
        out = out.reshape(rows, qcols)
    returned = lax.all_to_all(
        out.reshape(n_g, tok, qcols), "cg", split_axis=0, concat_axis=2, tiled=True
    )
    return returned.reshape(tok, n_g * qcols)


def solution(mesh):
    ctx = mesh.shape["ctx"]
    fsdp = mesh.shape["fsdp"]
    n_g = KV // fsdp
    n_t = ctx // n_g
    order = [mesh.axis_names.index("ctx"), mesh.axis_names.index("fsdp")]
    devices = np.transpose(mesh.devices, order).reshape(n_t, n_g, fsdp)
    grid = Mesh(devices, ("ct", "cg", "fsdp"))
    spec = P(("ct", "cg"), "fsdp")
    placed = (spec, spec, spec, spec, P(), P(), P())
    return jax.shard_map(shards, mesh=grid, in_specs=placed, out_specs=spec, check_vma=False)
```

```python
import jax
import jax.numpy as jnp
import numpy as np
from jax import lax
from jax.sharding import Mesh
from jax.sharding import PartitionSpec as P

HQ = 64
KV = 8
HD = 128


golden = -1640531535
drop_rate = 0.1
drop_level = 1677722
rope_theta = 500000.0
masked_score = -1e30


def shift_down(values, amount):
    return lax.shift_right_logical(values, jnp.full(values.shape, amount, jnp.int32))


def scramble(values):
    values = jnp.bitwise_xor(values, shift_down(values, 16))
    values = values * jnp.int32(-2048144789)
    values = jnp.bitwise_xor(values, shift_down(values, 13))
    values = values * jnp.int32(-1028477387)
    return jnp.bitwise_xor(values, shift_down(values, 16))


def head_word(seed_words, stream_offset, layer_index, head_ids):
    inner = scramble(head_ids + stream_offset[0])
    middle = scramble(layer_index[0] * jnp.int32(golden) + inner)
    return scramble(seed_words[0] + middle)


def rotation(positions):
    half_width = HD // 2
    exponent = jnp.arange(half_width, dtype=jnp.float32) * 2.0 / HD
    frequency = rope_theta ** (-exponent)
    angles = positions.astype(jnp.float32)[:, None] * frequency[None, :]
    return jnp.cos(angles), jnp.sin(angles)


def rotate(values, cosine, sine_part):
    half_width = HD // 2
    first_half = values[..., :half_width]
    second_half = values[..., half_width:]
    return jnp.concatenate(
        [
            first_half * cosine - second_half * sine_part,
            second_half * cosine + first_half * sine_part,
        ],
        axis=-1,
    )


def shards(activations, w_query, w_key, w_value, seed_words, stream_offset, layer_index):
    n_g = lax.axis_size("cg")
    n_t = lax.axis_size("ct")
    g = lax.axis_index("cg")
    t = lax.axis_index("ct")
    f = lax.axis_index("fsdp")
    tok = activations.shape[0]
    d_rows = w_query.shape[0]
    group_heads = HQ // KV
    local_heads = w_query.shape[1] // HD
    qcols = group_heads * HD
    rows = n_g * tok

    own_half = [activations]
    for shift in range(1, n_g):
        perm = [(i, (i + shift) % n_g) for i in range(n_g)]
        own_half.append(lax.ppermute(activations, "cg", perm))
    own_half = jnp.concatenate(own_half, axis=0)
    if lax.axis_size("fsdp") == 2:
        other_half = lax.ppermute(own_half, "fsdp", [(0, 1), (1, 0)])
        grp_rows = jnp.where(
            f == 0,
            jnp.concatenate([own_half, other_half], axis=1),
            jnp.concatenate([other_half, own_half], axis=1),
        )
    else:
        grp_rows = lax.all_gather(own_half, "fsdp", axis=1, tiled=True)

    local_w = jnp.concatenate(
        [
            w_query.reshape(d_rows, n_g, qcols),
            w_key.reshape(d_rows, n_g, HD),
            w_value.reshape(d_rows, n_g, HD),
        ],
        axis=2,
    )
    received = [lax.dynamic_index_in_dim(local_w, g, 1, keepdims=False)]
    for shift in range(1, n_g):
        outgoing = lax.dynamic_index_in_dim(local_w, (g + shift) % n_g, 1, keepdims=False)
        perm = [(i, (i + shift) % n_g) for i in range(n_g)]
        received.append(lax.ppermute(outgoing, "cg", perm))
    by_shift = jnp.stack(received, axis=0)
    back = (g - jnp.arange(n_g, dtype=jnp.int32)) % n_g
    mine = jnp.take(by_shift, back, axis=0)
    every = lax.all_gather(mine, "ct", axis=0, tiled=False)
    every = every.transpose(1, 0, 2, 3).reshape(n_g * n_t * d_rows, qcols + 2 * HD)

    mixed = jnp.dot(grp_rows, every, preferred_element_type=jnp.float32)
    mixed = jnp.take(mixed.reshape(n_g, tok, -1), back, axis=0).reshape(rows, -1)
    chunk_of_row = n_t * (jnp.arange(rows, dtype=jnp.int32) // tok) + t
    positions = chunk_of_row * tok + jnp.arange(rows, dtype=jnp.int32) % tok
    cosine, sine_part = rotation(positions)
    queries = rotate(
        mixed[:, :qcols].reshape(rows, group_heads, HD), cosine[:, None, :], sine_part[:, None, :]
    ).astype(jnp.bfloat16)
    keys = rotate(mixed[:, qcols : qcols + HD], cosine, sine_part).astype(jnp.bfloat16)
    values = mixed[:, qcols + HD :].astype(jnp.bfloat16)

    pair = jnp.stack([keys, values], axis=1)
    pair = lax.all_gather(pair, "ct", axis=0, tiled=False)
    pair = pair.reshape(n_t, n_g, tok, 2, HD).transpose(1, 0, 2, 3, 4)
    pair = pair.reshape(n_g * n_t * tok, 2, HD)
    all_keys = pair[:, 0]
    all_values = pair[:, 1]

    head_global = f * local_heads + g * group_heads + jnp.arange(group_heads, dtype=jnp.int32)
    words = head_word(seed_words, stream_offset, layer_index, head_global)
    score_scale = HD ** (-0.5)
    pieces = []
    for chunk in range(n_g):
        span = n_t * (chunk + 1) * tok
        query_pos = (n_t * chunk + t) * tok + jnp.arange(tok, dtype=jnp.int32)
        key_pos = jnp.arange(span, dtype=jnp.int32)
        chunk_queries = queries[chunk * tok : (chunk + 1) * tok]
        scores = (
            jnp.einsum(
                "qhe,ke->hqk",
                chunk_queries,
                all_keys[:span],
                preferred_element_type=jnp.float32,
            )
            * score_scale
        )
        visible = key_pos[None, None, :] <= query_pos[None, :, None]
        highest = jnp.max(jnp.where(visible, scores, masked_score), axis=2, keepdims=True)
        weights = jnp.where(visible, jnp.exp(scores - highest), 0.0)
        summed = jnp.sum(weights, axis=2)
        row_words = scramble(jnp.bitwise_xor(words[:, None], query_pos[None, :]))
        mixed_bits = scramble(row_words[:, :, None] + (key_pos * jnp.int32(golden))[None, None, :])
        keep = shift_down(mixed_bits, 8) >= drop_level
        dropped = jnp.where(keep, weights, 0.0).astype(jnp.bfloat16)
        attended = jnp.einsum(
            "hqk,ke->hqe", dropped, all_values[:span], preferred_element_type=jnp.float32
        )
        result = (attended / (summed * (1.0 - drop_rate))[:, :, None]).astype(jnp.bfloat16)
        pieces.append(result.transpose(1, 0, 2).reshape(tok, qcols))
    out_rows = jnp.stack(pieces, axis=0)
    returned = lax.all_to_all(out_rows, "cg", split_axis=0, concat_axis=2, tiled=True)
    return returned.reshape(tok, n_g * qcols)


def solution(mesh):
    ctx = mesh.shape["ctx"]
    fsdp = mesh.shape["fsdp"]
    n_g = KV // fsdp
    n_t = ctx // n_g
    order = [mesh.axis_names.index("ctx"), mesh.axis_names.index("fsdp")]
    devices = np.transpose(mesh.devices, order).reshape(n_g, n_t, fsdp)
    grid = Mesh(devices, ("cg", "ct", "fsdp"))
    spec = P(("cg", "ct"), "fsdp")
    placed = (spec, spec, spec, spec, P(), P(), P())
    return jax.shard_map(shards, mesh=grid, in_specs=placed, out_specs=spec, check_vma=False)
```

```python
import jax
import jax.numpy as jnp
import numpy as np
from jax import lax
from jax.sharding import Mesh
from jax.sharding import PartitionSpec as P

HQ = 64
KV = 8
HD = 128


golden = -1640531535
drop_rate = 0.1
drop_level = 1677722
rope_theta = 500000.0
masked_score = -1e30


def shift_down(values, amount):
    return lax.shift_right_logical(values, jnp.full(values.shape, amount, jnp.int32))


def scramble(values):
    values = jnp.bitwise_xor(values, shift_down(values, 16))
    values = values * jnp.int32(-2048144789)
    values = jnp.bitwise_xor(values, shift_down(values, 13))
    values = values * jnp.int32(-1028477387)
    return jnp.bitwise_xor(values, shift_down(values, 16))


def head_word(seed_words, stream_offset, layer_index, head_ids):
    inner = scramble(head_ids + stream_offset[0])
    middle = scramble(layer_index[0] * jnp.int32(golden) + inner)
    return scramble(seed_words[0] + middle)


def rotation(positions):
    half_width = HD // 2
    exponent = jnp.arange(half_width, dtype=jnp.float32) * 2.0 / HD
    frequency = rope_theta ** (-exponent)
    angles = positions.astype(jnp.float32)[:, None] * frequency[None, :]
    return jnp.cos(angles), jnp.sin(angles)


def rotate(values, cosine, sine_part):
    half_width = HD // 2
    first_half = values[..., :half_width]
    second_half = values[..., half_width:]
    return jnp.concatenate(
        [
            first_half * cosine - second_half * sine_part,
            second_half * cosine + first_half * sine_part,
        ],
        axis=-1,
    )


def shards(activations, w_query, w_key, w_value, seed_words, stream_offset, layer_index):
    n_g = lax.axis_size("cg")
    n_t = lax.axis_size("ct")
    g = lax.axis_index("cg")
    t = lax.axis_index("ct")
    f = lax.axis_index("fsdp")
    tok = activations.shape[0]
    d_rows = w_query.shape[0]
    group_heads = HQ // KV
    local_heads = w_query.shape[1] // HD
    qcols = group_heads * HD
    rows = n_g * tok

    if lax.axis_size("fsdp") == 2:
        other_half = lax.ppermute(activations, "fsdp", [(0, 1), (1, 0)])
        full_rows = jnp.where(
            f == 0,
            jnp.concatenate([activations, other_half], axis=1),
            jnp.concatenate([other_half, activations], axis=1),
        )
    else:
        full_rows = lax.all_gather(activations, "fsdp", axis=1, tiled=True)
    grp_rows = [full_rows]
    for shift in range(1, n_g):
        perm = [(i, (i + shift) % n_g) for i in range(n_g)]
        grp_rows.append(lax.ppermute(full_rows, "cg", perm))
    grp_rows = jnp.concatenate(grp_rows, axis=0)

    local_w = jnp.concatenate(
        [
            w_query.reshape(d_rows, n_g, qcols),
            w_key.reshape(d_rows, n_g, HD),
            w_value.reshape(d_rows, n_g, HD),
        ],
        axis=2,
    )
    received = [lax.dynamic_index_in_dim(local_w, g, 1, keepdims=False)]
    for shift in range(1, n_g):
        outgoing = lax.dynamic_index_in_dim(local_w, (g + shift) % n_g, 1, keepdims=False)
        perm = [(i, (i + shift) % n_g) for i in range(n_g)]
        received.append(lax.ppermute(outgoing, "cg", perm))
    by_shift = jnp.stack(received, axis=0)
    back = (g - jnp.arange(n_g, dtype=jnp.int32)) % n_g
    mine = jnp.take(by_shift, back, axis=0)
    every = lax.all_gather(mine, "ct", axis=0, tiled=False)
    every = every.transpose(1, 0, 2, 3).reshape(n_g * n_t * d_rows, qcols + 2 * HD)

    mixed = jnp.dot(grp_rows, every, preferred_element_type=jnp.float32)
    mixed = jnp.take(mixed.reshape(n_g, tok, -1), back, axis=0).reshape(rows, -1)
    chunk_of_row = n_t * (jnp.arange(rows, dtype=jnp.int32) // tok) + t
    positions = chunk_of_row * tok + jnp.arange(rows, dtype=jnp.int32) % tok
    cosine, sine_part = rotation(positions)
    queries = rotate(
        mixed[:, :qcols].reshape(rows, group_heads, HD), cosine[:, None, :], sine_part[:, None, :]
    ).astype(jnp.bfloat16)
    keys = rotate(mixed[:, qcols : qcols + HD], cosine, sine_part).astype(jnp.bfloat16)
    values = mixed[:, qcols + HD :].astype(jnp.bfloat16)

    pair = jnp.stack([keys, values], axis=1)
    pair = lax.all_gather(pair, "ct", axis=0, tiled=False)
    pair = pair.reshape(n_t, n_g, tok, 2, HD).transpose(1, 0, 2, 3, 4)
    pair = pair.reshape(n_g * n_t * tok, 2, HD)
    all_keys = pair[:, 0]
    all_values = pair[:, 1]

    head_global = f * local_heads + g * group_heads + jnp.arange(group_heads, dtype=jnp.int32)
    words = head_word(seed_words, stream_offset, layer_index, head_global)
    score_scale = HD ** (-0.5)
    pieces = []
    for chunk in range(n_g):
        span = n_t * (chunk + 1) * tok
        query_pos = (n_t * chunk + t) * tok + jnp.arange(tok, dtype=jnp.int32)
        key_pos = jnp.arange(span, dtype=jnp.int32)
        chunk_queries = queries[chunk * tok : (chunk + 1) * tok]
        scores = (
            jnp.einsum(
                "qhe,ke->hqk",
                chunk_queries,
                all_keys[:span],
                preferred_element_type=jnp.float32,
            )
            * score_scale
        )
        visible = key_pos[None, None, :] <= query_pos[None, :, None]
        highest = jnp.max(jnp.where(visible, scores, masked_score), axis=2, keepdims=True)
        weights = jnp.where(visible, jnp.exp(scores - highest), 0.0)
        summed = jnp.sum(weights, axis=2)
        row_words = scramble(jnp.bitwise_xor(words[:, None], query_pos[None, :]))
        mixed_bits = scramble(row_words[:, :, None] + (key_pos * jnp.int32(golden))[None, None, :])
        keep = shift_down(mixed_bits, 8) >= drop_level
        dropped = jnp.where(keep, weights, 0.0).astype(jnp.bfloat16)
        attended = jnp.einsum(
            "hqk,ke->hqe", dropped, all_values[:span], preferred_element_type=jnp.float32
        )
        result = (attended / (summed * (1.0 - drop_rate))[:, :, None]).astype(jnp.bfloat16)
        pieces.append(result.transpose(1, 0, 2).reshape(tok, qcols))
    out_rows = jnp.stack(pieces, axis=0)
    returned = lax.all_to_all(out_rows, "cg", split_axis=0, concat_axis=2, tiled=True)
    return returned.reshape(tok, n_g * qcols)


def solution(mesh):
    ctx = mesh.shape["ctx"]
    fsdp = mesh.shape["fsdp"]
    n_g = KV // fsdp
    n_t = ctx // n_g
    order = [mesh.axis_names.index("ctx"), mesh.axis_names.index("fsdp")]
    devices = np.transpose(mesh.devices, order).reshape(n_g, n_t, fsdp)
    grid = Mesh(devices, ("cg", "ct", "fsdp"))
    spec = P(("cg", "ct"), "fsdp")
    placed = (spec, spec, spec, spec, P(), P(), P())
    return jax.shard_map(shards, mesh=grid, in_specs=placed, out_specs=spec, check_vma=False)
```

```python
import jax
import jax.numpy as jnp
import numpy as np
from jax import lax
from jax.sharding import Mesh
from jax.sharding import PartitionSpec as P

HQ = 64
KV = 8
HD = 128


golden = -1640531535
drop_rate = 0.1
drop_level = 1677722
rope_theta = 500000.0
masked_score = -1e30


def shift_down(values, amount):
    return lax.shift_right_logical(values, jnp.full(values.shape, amount, jnp.int32))


def scramble(values):
    values = jnp.bitwise_xor(values, shift_down(values, 16))
    values = values * jnp.int32(-2048144789)
    values = jnp.bitwise_xor(values, shift_down(values, 13))
    values = values * jnp.int32(-1028477387)
    return jnp.bitwise_xor(values, shift_down(values, 16))


def head_word(seed_words, stream_offset, layer_index, head_ids):
    inner = scramble(head_ids + stream_offset[0])
    middle = scramble(layer_index[0] * jnp.int32(golden) + inner)
    return scramble(seed_words[0] + middle)


def rotation(positions):
    half_width = HD // 2
    exponent = jnp.arange(half_width, dtype=jnp.float32) * 2.0 / HD
    frequency = rope_theta ** (-exponent)
    angles = positions.astype(jnp.float32)[:, None] * frequency[None, :]
    return jnp.cos(angles), jnp.sin(angles)


def rotate(values, cosine, sine_part):
    half_width = HD // 2
    first_half = values[..., :half_width]
    second_half = values[..., half_width:]
    return jnp.concatenate(
        [
            first_half * cosine - second_half * sine_part,
            second_half * cosine + first_half * sine_part,
        ],
        axis=-1,
    )


def shards(activations, w_query, w_key, w_value, seed_words, stream_offset, layer_index):
    n_g = lax.axis_size("cg")
    n_t = lax.axis_size("ct")
    g = lax.axis_index("cg")
    t = lax.axis_index("ct")
    f = lax.axis_index("fsdp")
    tok = activations.shape[0]
    d_rows = w_query.shape[0]
    group_heads = HQ // KV
    local_heads = w_query.shape[1] // HD
    qcols = group_heads * HD
    rows = n_g * tok

    full_rows = lax.all_gather(activations, "fsdp", axis=1, tiled=True)
    grp_rows = lax.all_gather(full_rows, "cg", axis=0, tiled=True)

    local_w = jnp.concatenate(
        [
            w_query.reshape(d_rows, n_g, qcols),
            w_key.reshape(d_rows, n_g, HD),
            w_value.reshape(d_rows, n_g, HD),
        ],
        axis=2,
    )
    received = [lax.dynamic_index_in_dim(local_w, g, 1, keepdims=False)]
    for shift in range(1, n_g):
        outgoing = lax.dynamic_index_in_dim(local_w, (g + shift) % n_g, 1, keepdims=False)
        perm = [(i, (i + shift) % n_g) for i in range(n_g)]
        received.append(lax.ppermute(outgoing, "cg", perm))
    by_shift = jnp.stack(received, axis=0)
    back = (g - jnp.arange(n_g, dtype=jnp.int32)) % n_g
    mine = jnp.take(by_shift, back, axis=0)
    grp_rows, mine = lax.optimization_barrier((grp_rows, mine))
    every = lax.all_gather(mine, "ct", axis=0, tiled=False)
    every = every.transpose(1, 0, 2, 3).reshape(n_g * n_t * d_rows, qcols + 2 * HD)

    mixed = jnp.dot(grp_rows, every, preferred_element_type=jnp.float32)
    chunk_of_row = n_t * (jnp.arange(rows, dtype=jnp.int32) // tok) + t
    positions = chunk_of_row * tok + jnp.arange(rows, dtype=jnp.int32) % tok
    cosine, sine_part = rotation(positions)
    queries = rotate(
        mixed[:, :qcols].reshape(rows, group_heads, HD), cosine[:, None, :], sine_part[:, None, :]
    ).astype(jnp.bfloat16)
    keys = rotate(mixed[:, qcols : qcols + HD], cosine, sine_part).astype(jnp.bfloat16)
    values = mixed[:, qcols + HD :].astype(jnp.bfloat16)

    pair = jnp.stack([keys, values], axis=1)
    pair = lax.all_gather(pair, "ct", axis=0, tiled=False)
    pair = pair.reshape(n_t, n_g, tok, 2, HD).transpose(1, 0, 2, 3, 4)
    pair = pair.reshape(n_g * n_t * tok, 2, HD)
    all_keys = pair[:, 0]
    all_values = pair[:, 1]

    head_global = f * local_heads + g * group_heads + jnp.arange(group_heads, dtype=jnp.int32)
    words = head_word(seed_words, stream_offset, layer_index, head_global)
    score_scale = HD ** (-0.5)
    pieces = []
    for chunk in range(n_g):
        span = n_t * (chunk + 1) * tok
        query_pos = (n_t * chunk + t) * tok + jnp.arange(tok, dtype=jnp.int32)
        key_pos = jnp.arange(span, dtype=jnp.int32)
        chunk_queries = queries[chunk * tok : (chunk + 1) * tok]
        scores = (
            jnp.einsum(
                "qhe,ke->hqk",
                chunk_queries,
                all_keys[:span],
                preferred_element_type=jnp.float32,
            )
            * score_scale
        )
        visible = key_pos[None, None, :] <= query_pos[None, :, None]
        highest = jnp.max(jnp.where(visible, scores, masked_score), axis=2, keepdims=True)
        weights = jnp.where(visible, jnp.exp(scores - highest), 0.0)
        summed = jnp.sum(weights, axis=2)
        row_words = scramble(jnp.bitwise_xor(words[:, None], query_pos[None, :]))
        mixed_bits = scramble(row_words[:, :, None] + (key_pos * jnp.int32(golden))[None, None, :])
        keep = shift_down(mixed_bits, 8) >= drop_level
        dropped = jnp.where(keep, weights, 0.0).astype(jnp.bfloat16)
        attended = jnp.einsum(
            "hqk,ke->hqe", dropped, all_values[:span], preferred_element_type=jnp.float32
        )
        result = (attended / (summed * (1.0 - drop_rate))[:, :, None]).astype(jnp.bfloat16)
        pieces.append(result.transpose(1, 0, 2).reshape(tok, qcols))
    out_rows = jnp.stack(pieces, axis=0)
    returned = lax.all_to_all(out_rows, "cg", split_axis=0, concat_axis=2, tiled=True)
    return returned.reshape(tok, n_g * qcols)


def solution(mesh):
    ctx = mesh.shape["ctx"]
    fsdp = mesh.shape["fsdp"]
    n_g = KV // fsdp
    n_t = ctx // n_g
    order = [mesh.axis_names.index("ctx"), mesh.axis_names.index("fsdp")]
    devices = np.transpose(mesh.devices, order).reshape(n_g, n_t, fsdp)
    grid = Mesh(devices, ("cg", "ct", "fsdp"))
    spec = P(("cg", "ct"), "fsdp")
    placed = (spec, spec, spec, spec, P(), P(), P())
    return jax.shard_map(shards, mesh=grid, in_specs=placed, out_specs=spec, check_vma=False)
```

```python
import jax
import jax.numpy as jnp
import numpy as np
from jax import lax
from jax.sharding import Mesh
from jax.sharding import PartitionSpec as P

HQ = 64
KV = 8
HD = 128


golden = -1640531535
drop_rate = 0.1
drop_level = 1677722
rope_theta = 500000.0
masked_score = -1e30


def shift_down(values, amount):
    return lax.shift_right_logical(values, jnp.full(values.shape, amount, jnp.int32))


def scramble(values):
    values = jnp.bitwise_xor(values, shift_down(values, 16))
    values = values * jnp.int32(-2048144789)
    values = jnp.bitwise_xor(values, shift_down(values, 13))
    values = values * jnp.int32(-1028477387)
    return jnp.bitwise_xor(values, shift_down(values, 16))


def head_word(seed_words, stream_offset, layer_index, head_ids):
    inner = scramble(head_ids + stream_offset[0])
    middle = scramble(layer_index[0] * jnp.int32(golden) + inner)
    return scramble(seed_words[0] + middle)


def rotation(positions):
    half_width = HD // 2
    exponent = jnp.arange(half_width, dtype=jnp.float32) * 2.0 / HD
    frequency = rope_theta ** (-exponent)
    angles = positions.astype(jnp.float32)[:, None] * frequency[None, :]
    return jnp.cos(angles), jnp.sin(angles)


def rotate(values, cosine, sine_part):
    half_width = HD // 2
    first_half = values[..., :half_width]
    second_half = values[..., half_width:]
    return jnp.concatenate(
        [
            first_half * cosine - second_half * sine_part,
            second_half * cosine + first_half * sine_part,
        ],
        axis=-1,
    )


def shards(activations, w_query, w_key, w_value, seed_words, stream_offset, layer_index):
    n_g = lax.axis_size("cg")
    n_t = lax.axis_size("ct")
    g = lax.axis_index("cg")
    t = lax.axis_index("ct")
    f = lax.axis_index("fsdp")
    tok = activations.shape[0]
    d_rows = w_query.shape[0]
    group_heads = HQ // KV
    local_heads = w_query.shape[1] // HD
    qcols = group_heads * HD
    rows = n_g * tok

    full_rows = lax.all_gather(activations, "fsdp", axis=1, tiled=True)

    local_w = jnp.concatenate(
        [
            w_query.reshape(d_rows, n_g, qcols),
            w_key.reshape(d_rows, n_g, HD),
            w_value.reshape(d_rows, n_g, HD),
        ],
        axis=2,
    )
    received = [lax.dynamic_index_in_dim(local_w, g, 1, keepdims=False)]
    for shift in range(1, n_g):
        outgoing = lax.dynamic_index_in_dim(local_w, (g + shift) % n_g, 1, keepdims=False)
        perm = [(i, (i + shift) % n_g) for i in range(n_g)]
        received.append(lax.ppermute(outgoing, "cg", perm))
    by_shift = jnp.stack(received, axis=0)
    back = (g - jnp.arange(n_g, dtype=jnp.int32)) % n_g
    mine = jnp.take(by_shift, back, axis=0)
    full_rows, mine = lax.optimization_barrier((full_rows, mine))
    every = lax.all_gather(mine, "ct", axis=0, tiled=False)
    full_rows, every = lax.optimization_barrier((full_rows, every))
    grp_rows = lax.all_gather(full_rows, "cg", axis=0, tiled=True)
    every = every.transpose(1, 0, 2, 3).reshape(n_g * n_t * d_rows, qcols + 2 * HD)

    mixed = jnp.dot(grp_rows, every, preferred_element_type=jnp.float32)
    chunk_of_row = n_t * (jnp.arange(rows, dtype=jnp.int32) // tok) + t
    positions = chunk_of_row * tok + jnp.arange(rows, dtype=jnp.int32) % tok
    cosine, sine_part = rotation(positions)
    queries = rotate(
        mixed[:, :qcols].reshape(rows, group_heads, HD), cosine[:, None, :], sine_part[:, None, :]
    ).astype(jnp.bfloat16)
    keys = rotate(mixed[:, qcols : qcols + HD], cosine, sine_part).astype(jnp.bfloat16)
    values = mixed[:, qcols + HD :].astype(jnp.bfloat16)

    pair = jnp.stack([keys, values], axis=1)
    pair = lax.all_gather(pair, "ct", axis=0, tiled=False)
    pair = pair.reshape(n_t, n_g, tok, 2, HD).transpose(1, 0, 2, 3, 4)
    pair = pair.reshape(n_g * n_t * tok, 2, HD)
    all_keys = pair[:, 0]
    all_values = pair[:, 1]

    head_global = f * local_heads + g * group_heads + jnp.arange(group_heads, dtype=jnp.int32)
    words = head_word(seed_words, stream_offset, layer_index, head_global)
    score_scale = HD ** (-0.5)
    pieces = []
    for chunk in range(n_g):
        span = n_t * (chunk + 1) * tok
        query_pos = (n_t * chunk + t) * tok + jnp.arange(tok, dtype=jnp.int32)
        key_pos = jnp.arange(span, dtype=jnp.int32)
        chunk_queries = queries[chunk * tok : (chunk + 1) * tok]
        scores = (
            jnp.einsum(
                "qhe,ke->hqk",
                chunk_queries,
                all_keys[:span],
                preferred_element_type=jnp.float32,
            )
            * score_scale
        )
        visible = key_pos[None, None, :] <= query_pos[None, :, None]
        highest = jnp.max(jnp.where(visible, scores, masked_score), axis=2, keepdims=True)
        weights = jnp.where(visible, jnp.exp(scores - highest), 0.0)
        summed = jnp.sum(weights, axis=2)
        row_words = scramble(jnp.bitwise_xor(words[:, None], query_pos[None, :]))
        mixed_bits = scramble(row_words[:, :, None] + (key_pos * jnp.int32(golden))[None, None, :])
        keep = shift_down(mixed_bits, 8) >= drop_level
        dropped = jnp.where(keep, weights, 0.0).astype(jnp.bfloat16)
        attended = jnp.einsum(
            "hqk,ke->hqe", dropped, all_values[:span], preferred_element_type=jnp.float32
        )
        result = (attended / (summed * (1.0 - drop_rate))[:, :, None]).astype(jnp.bfloat16)
        pieces.append(result.transpose(1, 0, 2).reshape(tok, qcols))
    out_rows = jnp.stack(pieces, axis=0)
    returned = lax.all_to_all(out_rows, "cg", split_axis=0, concat_axis=2, tiled=True)
    return returned.reshape(tok, n_g * qcols)


def solution(mesh):
    ctx = mesh.shape["ctx"]
    fsdp = mesh.shape["fsdp"]
    n_g = KV // fsdp
    n_t = ctx // n_g
    order = [mesh.axis_names.index("ctx"), mesh.axis_names.index("fsdp")]
    devices = np.transpose(mesh.devices, order).reshape(n_g, n_t, fsdp)
    grid = Mesh(devices, ("cg", "ct", "fsdp"))
    spec = P(("cg", "ct"), "fsdp")
    placed = (spec, spec, spec, spec, P(), P(), P())
    return jax.shard_map(shards, mesh=grid, in_specs=placed, out_specs=spec, check_vma=False)
```

```python
import jax
import jax.numpy as jnp
import numpy as np
from jax import lax
from jax.sharding import Mesh
from jax.sharding import PartitionSpec as P

HQ = 64
KV = 8
HD = 128


golden = -1640531535
drop_rate = 0.1
drop_level = 1677722
rope_theta = 500000.0
masked_score = -1e30


def shift_down(values, amount):
    return lax.shift_right_logical(values, jnp.full(values.shape, amount, jnp.int32))


def scramble(values):
    values = jnp.bitwise_xor(values, shift_down(values, 16))
    values = values * jnp.int32(-2048144789)
    values = jnp.bitwise_xor(values, shift_down(values, 13))
    values = values * jnp.int32(-1028477387)
    return jnp.bitwise_xor(values, shift_down(values, 16))


def head_word(seed_words, stream_offset, layer_index, head_ids):
    inner = scramble(head_ids + stream_offset[0])
    middle = scramble(layer_index[0] * jnp.int32(golden) + inner)
    return scramble(seed_words[0] + middle)


def rotation(positions):
    half_width = HD // 2
    exponent = jnp.arange(half_width, dtype=jnp.float32) * 2.0 / HD
    frequency = rope_theta ** (-exponent)
    angles = positions.astype(jnp.float32)[:, None] * frequency[None, :]
    return jnp.cos(angles), jnp.sin(angles)


def rotate(values, cosine, sine_part):
    half_width = HD // 2
    first_half = values[..., :half_width]
    second_half = values[..., half_width:]
    return jnp.concatenate(
        [
            first_half * cosine - second_half * sine_part,
            second_half * cosine + first_half * sine_part,
        ],
        axis=-1,
    )


def shards(activations, w_query, w_key, w_value, seed_words, stream_offset, layer_index):
    n_g = lax.axis_size("cg")
    n_t = lax.axis_size("ct")
    g = lax.axis_index("cg")
    t = lax.axis_index("ct")
    f = lax.axis_index("fsdp")
    tok = activations.shape[0]
    d_rows = w_query.shape[0]
    group_heads = HQ // KV
    local_heads = w_query.shape[1] // HD
    qcols = group_heads * HD
    rows = n_g * tok

    local_w = jnp.concatenate(
        [
            w_query.reshape(d_rows, n_g, qcols),
            w_key.reshape(d_rows, n_g, HD),
            w_value.reshape(d_rows, n_g, HD),
        ],
        axis=2,
    )
    received = [lax.dynamic_index_in_dim(local_w, g, 1, keepdims=False)]
    for shift in range(1, n_g):
        outgoing = lax.dynamic_index_in_dim(local_w, (g + shift) % n_g, 1, keepdims=False)
        perm = [(i, (i + shift) % n_g) for i in range(n_g)]
        received.append(lax.ppermute(outgoing, "cg", perm))
    by_shift = jnp.stack(received, axis=0)
    back = (g - jnp.arange(n_g, dtype=jnp.int32)) % n_g
    mine = jnp.take(by_shift, back, axis=0)

    if lax.axis_size("fsdp") == 2:
        other_half = lax.ppermute(activations, "fsdp", [(0, 1), (1, 0)])
        full_rows = jnp.where(
            f == 0,
            jnp.concatenate([activations, other_half], axis=1),
            jnp.concatenate([other_half, activations], axis=1),
        )
    else:
        full_rows = lax.all_gather(activations, "fsdp", axis=1, tiled=True)
    grp_rows = [full_rows]
    full_rows, mine = lax.optimization_barrier((full_rows, mine))
    for shift in range(1, n_g):
        perm = [(i, (i + shift) % n_g) for i in range(n_g)]
        grp_rows.append(lax.ppermute(full_rows, "cg", perm))
    grp_rows = jnp.concatenate(grp_rows, axis=0)

    every = lax.all_gather(mine, "ct", axis=0, tiled=False)

    mixed = jnp.einsum(
        "rgtd,tgdc->rc",
        grp_rows.reshape(rows, n_g, n_t, d_rows),
        every,
        preferred_element_type=jnp.float32,
    )
    mixed = jnp.take(mixed.reshape(n_g, tok, -1), back, axis=0).reshape(rows, -1)
    chunk_of_row = n_t * (jnp.arange(rows, dtype=jnp.int32) // tok) + t
    positions = chunk_of_row * tok + jnp.arange(rows, dtype=jnp.int32) % tok
    cosine, sine_part = rotation(positions)
    queries = rotate(
        mixed[:, :qcols].reshape(rows, group_heads, HD), cosine[:, None, :], sine_part[:, None, :]
    ).astype(jnp.bfloat16)
    keys = rotate(mixed[:, qcols : qcols + HD], cosine, sine_part).astype(jnp.bfloat16)
    values = mixed[:, qcols + HD :].astype(jnp.bfloat16)

    pair = jnp.stack([keys, values], axis=1)
    pair = lax.all_gather(pair, "ct", axis=0, tiled=False)
    pair = pair.reshape(n_t, n_g, tok, 2, HD).transpose(1, 0, 2, 3, 4)
    pair = pair.reshape(n_g * n_t * tok, 2, HD)
    all_keys = pair[:, 0]
    all_values = pair[:, 1]

    head_global = f * local_heads + g * group_heads + jnp.arange(group_heads, dtype=jnp.int32)
    words = head_word(seed_words, stream_offset, layer_index, head_global)
    score_scale = HD ** (-0.5)
    pieces = []
    for chunk in range(n_g):
        span = n_t * (chunk + 1) * tok
        query_pos = (n_t * chunk + t) * tok + jnp.arange(tok, dtype=jnp.int32)
        key_pos = jnp.arange(span, dtype=jnp.int32)
        chunk_queries = queries[chunk * tok : (chunk + 1) * tok]
        scores = (
            jnp.einsum(
                "qhe,ke->hqk",
                chunk_queries,
                all_keys[:span],
                preferred_element_type=jnp.float32,
            )
            * score_scale
        )
        visible = key_pos[None, None, :] <= query_pos[None, :, None]
        highest = jnp.max(jnp.where(visible, scores, masked_score), axis=2, keepdims=True)
        weights = jnp.where(visible, jnp.exp(scores - highest), 0.0)
        summed = jnp.sum(weights, axis=2)
        row_words = scramble(jnp.bitwise_xor(words[:, None], query_pos[None, :]))
        mixed_bits = scramble(row_words[:, :, None] + (key_pos * jnp.int32(golden))[None, None, :])
        keep = shift_down(mixed_bits, 8) >= drop_level
        dropped = jnp.where(keep, weights, 0.0).astype(jnp.bfloat16)
        attended = jnp.einsum(
            "hqk,ke->hqe", dropped, all_values[:span], preferred_element_type=jnp.float32
        )
        result = (attended / (summed * (1.0 - drop_rate))[:, :, None]).astype(jnp.bfloat16)
        pieces.append(result.transpose(1, 0, 2).reshape(tok, qcols))
    out_rows = jnp.stack(pieces, axis=0)
    returned = lax.all_to_all(out_rows, "cg", split_axis=0, concat_axis=2, tiled=True)
    return returned.reshape(tok, n_g * qcols)


def solution(mesh):
    ctx = mesh.shape["ctx"]
    fsdp = mesh.shape["fsdp"]
    n_g = KV // fsdp
    n_t = ctx // n_g
    order = [mesh.axis_names.index("ctx"), mesh.axis_names.index("fsdp")]
    devices = np.transpose(mesh.devices, order).reshape(n_g, n_t, fsdp)
    grid = Mesh(devices, ("cg", "ct", "fsdp"))
    spec = P(("cg", "ct"), "fsdp")
    placed = (spec, spec, spec, spec, P(), P(), P())
    return jax.shard_map(shards, mesh=grid, in_specs=placed, out_specs=spec, check_vma=False)
```

```python
import jax
import jax.numpy as jnp
import numpy as np
from jax import lax
from jax.sharding import Mesh
from jax.sharding import PartitionSpec as P

HQ = 64
KV = 8
HD = 128


golden = -1640531535
drop_rate = 0.1
drop_level = 1677722
rope_theta = 500000.0
masked_score = -1e30


def shift_down(values, amount):
    return lax.shift_right_logical(values, jnp.full(values.shape, amount, jnp.int32))


def scramble(values):
    values = jnp.bitwise_xor(values, shift_down(values, 16))
    values = values * jnp.int32(-2048144789)
    values = jnp.bitwise_xor(values, shift_down(values, 13))
    values = values * jnp.int32(-1028477387)
    return jnp.bitwise_xor(values, shift_down(values, 16))


def head_word(seed_words, stream_offset, layer_index, head_ids):
    inner = scramble(head_ids + stream_offset[0])
    middle = scramble(layer_index[0] * jnp.int32(golden) + inner)
    return scramble(seed_words[0] + middle)


def rotation(positions):
    half_width = HD // 2
    exponent = jnp.arange(half_width, dtype=jnp.float32) * 2.0 / HD
    frequency = rope_theta ** (-exponent)
    angles = positions.astype(jnp.float32)[:, None] * frequency[None, :]
    return jnp.cos(angles), jnp.sin(angles)


def rotate(values, cosine, sine_part):
    half_width = HD // 2
    first_half = values[..., :half_width]
    second_half = values[..., half_width:]
    return jnp.concatenate(
        [
            first_half * cosine - second_half * sine_part,
            second_half * cosine + first_half * sine_part,
        ],
        axis=-1,
    )


def shards(activations, w_query, w_key, w_value, seed_words, stream_offset, layer_index):
    n_g = lax.axis_size("cg")
    n_t = lax.axis_size("ct")
    g = lax.axis_index("cg")
    t = lax.axis_index("ct")
    f = lax.axis_index("fsdp")
    tok = activations.shape[0]
    d_rows = w_query.shape[0]
    group_heads = HQ // KV
    local_heads = w_query.shape[1] // HD
    qcols = group_heads * HD
    rows = n_g * tok

    if lax.axis_size("fsdp") == 2:
        pieces = []
        for shift in range(n_g):
            if shift:
                perm = [(i, (i + shift) % n_g) for i in range(n_g)]
                mine_half = lax.ppermute(activations, "cg", perm)
            else:
                mine_half = activations
            other_half = lax.ppermute(mine_half, "fsdp", [(0, 1), (1, 0)])
            pieces.append(
                jnp.where(
                    f == 0,
                    jnp.concatenate([mine_half, other_half], axis=1),
                    jnp.concatenate([other_half, mine_half], axis=1),
                )
            )
        grp_rows = jnp.concatenate(pieces, axis=0)
    else:
        own_half = [activations]
        for shift in range(1, n_g):
            perm = [(i, (i + shift) % n_g) for i in range(n_g)]
            own_half.append(lax.ppermute(activations, "cg", perm))
        grp_rows = lax.all_gather(jnp.concatenate(own_half, axis=0), "fsdp", axis=1, tiled=True)

    local_w = jnp.concatenate(
        [
            w_query.reshape(d_rows, n_g, qcols),
            w_key.reshape(d_rows, n_g, HD),
            w_value.reshape(d_rows, n_g, HD),
        ],
        axis=2,
    )
    received = [lax.dynamic_index_in_dim(local_w, g, 1, keepdims=False)]
    for shift in range(1, n_g):
        outgoing = lax.dynamic_index_in_dim(local_w, (g + shift) % n_g, 1, keepdims=False)
        perm = [(i, (i + shift) % n_g) for i in range(n_g)]
        received.append(lax.ppermute(outgoing, "cg", perm))
    by_shift = jnp.stack(received, axis=0)
    back = (g - jnp.arange(n_g, dtype=jnp.int32)) % n_g
    mine = jnp.take(by_shift, back, axis=0)
    every = lax.all_gather(mine, "ct", axis=0, tiled=False)
    every = every.transpose(1, 0, 2, 3).reshape(n_g * n_t * d_rows, qcols + 2 * HD)

    mixed = jnp.dot(grp_rows, every, preferred_element_type=jnp.float32)
    mixed = jnp.take(mixed.reshape(n_g, tok, -1), back, axis=0).reshape(rows, -1)
    chunk_of_row = n_t * (jnp.arange(rows, dtype=jnp.int32) // tok) + t
    positions = chunk_of_row * tok + jnp.arange(rows, dtype=jnp.int32) % tok
    cosine, sine_part = rotation(positions)
    queries = rotate(
        mixed[:, :qcols].reshape(rows, group_heads, HD), cosine[:, None, :], sine_part[:, None, :]
    ).astype(jnp.bfloat16)
    keys = rotate(mixed[:, qcols : qcols + HD], cosine, sine_part).astype(jnp.bfloat16)
    values = mixed[:, qcols + HD :].astype(jnp.bfloat16)

    pair = jnp.stack([keys, values], axis=1)
    pair = lax.all_gather(pair, "ct", axis=0, tiled=False)
    pair = pair.reshape(n_t, n_g, tok, 2, HD).transpose(1, 0, 2, 3, 4)
    pair = pair.reshape(n_g * n_t * tok, 2, HD)
    all_keys = pair[:, 0]
    all_values = pair[:, 1]

    head_global = f * local_heads + g * group_heads + jnp.arange(group_heads, dtype=jnp.int32)
    words = head_word(seed_words, stream_offset, layer_index, head_global)
    score_scale = HD ** (-0.5)
    pieces = []
    for chunk in range(n_g):
        span = n_t * (chunk + 1) * tok
        query_pos = (n_t * chunk + t) * tok + jnp.arange(tok, dtype=jnp.int32)
        key_pos = jnp.arange(span, dtype=jnp.int32)
        chunk_queries = queries[chunk * tok : (chunk + 1) * tok]
        scores = (
            jnp.einsum(
                "qhe,ke->hqk",
                chunk_queries,
                all_keys[:span],
                preferred_element_type=jnp.float32,
            )
            * score_scale
        )
        visible = key_pos[None, None, :] <= query_pos[None, :, None]
        highest = jnp.max(jnp.where(visible, scores, masked_score), axis=2, keepdims=True)
        weights = jnp.where(visible, jnp.exp(scores - highest), 0.0)
        summed = jnp.sum(weights, axis=2)
        row_words = scramble(jnp.bitwise_xor(words[:, None], query_pos[None, :]))
        mixed_bits = scramble(row_words[:, :, None] + (key_pos * jnp.int32(golden))[None, None, :])
        keep = shift_down(mixed_bits, 8) >= drop_level
        dropped = jnp.where(keep, weights, 0.0).astype(jnp.bfloat16)
        attended = jnp.einsum(
            "hqk,ke->hqe", dropped, all_values[:span], preferred_element_type=jnp.float32
        )
        result = (attended / (summed * (1.0 - drop_rate))[:, :, None]).astype(jnp.bfloat16)
        pieces.append(result.transpose(1, 0, 2).reshape(tok, qcols))
    out_rows = jnp.stack(pieces, axis=0)
    returned = lax.all_to_all(out_rows, "cg", split_axis=0, concat_axis=2, tiled=True)
    return returned.reshape(tok, n_g * qcols)


def solution(mesh):
    ctx = mesh.shape["ctx"]
    fsdp = mesh.shape["fsdp"]
    n_g = KV // fsdp
    n_t = ctx // n_g
    order = [mesh.axis_names.index("ctx"), mesh.axis_names.index("fsdp")]
    devices = np.transpose(mesh.devices, order).reshape(n_g, n_t, fsdp)
    grid = Mesh(devices, ("cg", "ct", "fsdp"))
    spec = P(("cg", "ct"), "fsdp")
    placed = (spec, spec, spec, spec, P(), P(), P())
    return jax.shard_map(shards, mesh=grid, in_specs=placed, out_specs=spec, check_vma=False)
```

```python
import jax
import jax.numpy as jnp
import numpy as np
from jax import lax
from jax.sharding import Mesh
from jax.sharding import PartitionSpec as P

HQ = 64
KV = 8
HD = 128


golden = -1640531535
drop_rate = 0.1
drop_level = 1677722
rope_theta = 500000.0
masked_score = -1e30


def shift_down(values, amount):
    return lax.shift_right_logical(values, jnp.full(values.shape, amount, jnp.int32))


def scramble(values):
    values = jnp.bitwise_xor(values, shift_down(values, 16))
    values = values * jnp.int32(-2048144789)
    values = jnp.bitwise_xor(values, shift_down(values, 13))
    values = values * jnp.int32(-1028477387)
    return jnp.bitwise_xor(values, shift_down(values, 16))


def head_word(seed_words, stream_offset, layer_index, head_ids):
    inner = scramble(head_ids + stream_offset[0])
    middle = scramble(layer_index[0] * jnp.int32(golden) + inner)
    return scramble(seed_words[0] + middle)


def rotation(positions):
    half_width = HD // 2
    exponent = jnp.arange(half_width, dtype=jnp.float32) * 2.0 / HD
    frequency = rope_theta ** (-exponent)
    angles = positions.astype(jnp.float32)[:, None] * frequency[None, :]
    return jnp.cos(angles), jnp.sin(angles)


def rotate(values, cosine, sine_part):
    half_width = HD // 2
    first_half = values[..., :half_width]
    second_half = values[..., half_width:]
    return jnp.concatenate(
        [
            first_half * cosine - second_half * sine_part,
            second_half * cosine + first_half * sine_part,
        ],
        axis=-1,
    )


def shards(activations, w_query, w_key, w_value, seed_words, stream_offset, layer_index):
    n_g = lax.axis_size("cg")
    n_t = lax.axis_size("ct")
    g = lax.axis_index("cg")
    t = lax.axis_index("ct")
    f = lax.axis_index("fsdp")
    tok = activations.shape[0]
    d_rows = w_query.shape[0]
    group_heads = HQ // KV
    local_heads = w_query.shape[1] // HD
    qcols = group_heads * HD
    rows = n_g * tok

    if lax.axis_size("fsdp") == 2:
        pieces = []
        halves = [activations]
        if n_g == 4:
            right = [(i, (i + 1) % n_g) for i in range(n_g)]
            left = [(i, (i - 1) % n_g) for i in range(n_g)]
            from_left = lax.ppermute(activations, "cg", right)
            from_right = lax.ppermute(activations, "cg", left)
            halves += [from_left, lax.ppermute(from_left, "cg", right), from_right]
        else:
            for shift in range(1, n_g):
                perm = [(i, (i + shift) % n_g) for i in range(n_g)]
                halves.append(lax.ppermute(activations, "cg", perm))
        for mine_half in halves:
            other_half = lax.ppermute(mine_half, "fsdp", [(0, 1), (1, 0)])
            pieces.append(
                jnp.where(
                    f == 0,
                    jnp.concatenate([mine_half, other_half], axis=1),
                    jnp.concatenate([other_half, mine_half], axis=1),
                )
            )
        grp_rows = jnp.concatenate(pieces, axis=0)
    else:
        own_half = [activations]
        for shift in range(1, n_g):
            perm = [(i, (i + shift) % n_g) for i in range(n_g)]
            own_half.append(lax.ppermute(activations, "cg", perm))
        grp_rows = lax.all_gather(jnp.concatenate(own_half, axis=0), "fsdp", axis=1, tiled=True)

    local_w = jnp.concatenate(
        [
            w_query.reshape(d_rows, n_g, qcols),
            w_key.reshape(d_rows, n_g, HD),
            w_value.reshape(d_rows, n_g, HD),
        ],
        axis=2,
    )
    received = [lax.dynamic_index_in_dim(local_w, g, 1, keepdims=False)]
    for shift in range(1, n_g):
        outgoing = lax.dynamic_index_in_dim(local_w, (g + shift) % n_g, 1, keepdims=False)
        perm = [(i, (i + shift) % n_g) for i in range(n_g)]
        received.append(lax.ppermute(outgoing, "cg", perm))
    by_shift = jnp.stack(received, axis=0)
    back = (g - jnp.arange(n_g, dtype=jnp.int32)) % n_g
    mine = jnp.take(by_shift, back, axis=0)
    every = lax.all_gather(mine, "ct", axis=0, tiled=False)
    every = every.transpose(1, 0, 2, 3).reshape(n_g * n_t * d_rows, qcols + 2 * HD)

    mixed = jnp.dot(grp_rows, every, preferred_element_type=jnp.float32)
    mixed = jnp.take(mixed.reshape(n_g, tok, -1), back, axis=0).reshape(rows, -1)
    chunk_of_row = n_t * (jnp.arange(rows, dtype=jnp.int32) // tok) + t
    positions = chunk_of_row * tok + jnp.arange(rows, dtype=jnp.int32) % tok
    cosine, sine_part = rotation(positions)
    queries = rotate(
        mixed[:, :qcols].reshape(rows, group_heads, HD), cosine[:, None, :], sine_part[:, None, :]
    ).astype(jnp.bfloat16)
    keys = rotate(mixed[:, qcols : qcols + HD], cosine, sine_part).astype(jnp.bfloat16)
    values = mixed[:, qcols + HD :].astype(jnp.bfloat16)

    pair = jnp.stack([keys, values], axis=1)
    pair = lax.all_gather(pair, "ct", axis=0, tiled=False)
    pair = pair.reshape(n_t, n_g, tok, 2, HD).transpose(1, 0, 2, 3, 4)
    pair = pair.reshape(n_g * n_t * tok, 2, HD)
    all_keys = pair[:, 0]
    all_values = pair[:, 1]

    head_global = f * local_heads + g * group_heads + jnp.arange(group_heads, dtype=jnp.int32)
    words = head_word(seed_words, stream_offset, layer_index, head_global)
    score_scale = HD ** (-0.5)
    pieces = []
    for chunk in range(n_g):
        span = n_t * (chunk + 1) * tok
        query_pos = (n_t * chunk + t) * tok + jnp.arange(tok, dtype=jnp.int32)
        key_pos = jnp.arange(span, dtype=jnp.int32)
        chunk_queries = queries[chunk * tok : (chunk + 1) * tok]
        scores = (
            jnp.einsum(
                "qhe,ke->hqk",
                chunk_queries,
                all_keys[:span],
                preferred_element_type=jnp.float32,
            )
            * score_scale
        )
        visible = key_pos[None, None, :] <= query_pos[None, :, None]
        highest = jnp.max(jnp.where(visible, scores, masked_score), axis=2, keepdims=True)
        weights = jnp.where(visible, jnp.exp(scores - highest), 0.0)
        summed = jnp.sum(weights, axis=2)
        row_words = scramble(jnp.bitwise_xor(words[:, None], query_pos[None, :]))
        mixed_bits = scramble(row_words[:, :, None] + (key_pos * jnp.int32(golden))[None, None, :])
        keep = shift_down(mixed_bits, 8) >= drop_level
        dropped = jnp.where(keep, weights, 0.0).astype(jnp.bfloat16)
        attended = jnp.einsum(
            "hqk,ke->hqe", dropped, all_values[:span], preferred_element_type=jnp.float32
        )
        result = (attended / (summed * (1.0 - drop_rate))[:, :, None]).astype(jnp.bfloat16)
        pieces.append(result.transpose(1, 0, 2).reshape(tok, qcols))
    out_rows = jnp.stack(pieces, axis=0)
    returned = lax.all_to_all(out_rows, "cg", split_axis=0, concat_axis=2, tiled=True)
    return returned.reshape(tok, n_g * qcols)


def solution(mesh):
    ctx = mesh.shape["ctx"]
    fsdp = mesh.shape["fsdp"]
    n_g = KV // fsdp
    n_t = ctx // n_g
    order = [mesh.axis_names.index("ctx"), mesh.axis_names.index("fsdp")]
    devices = np.transpose(mesh.devices, order).reshape(n_g, n_t, fsdp)
    grid = Mesh(devices, ("cg", "ct", "fsdp"))
    spec = P(("cg", "ct"), "fsdp")
    placed = (spec, spec, spec, spec, P(), P(), P())
    return jax.shard_map(shards, mesh=grid, in_specs=placed, out_specs=spec, check_vma=False)
```

```python
import jax
import jax.numpy as jnp
import numpy as np
from jax import lax
from jax.sharding import Mesh
from jax.sharding import PartitionSpec as P

HQ = 64
KV = 8
HD = 128


golden = -1640531535
drop_rate = 0.1
drop_level = 1677722
rope_theta = 500000.0
masked_score = -1e30


def shift_down(values, amount):
    return lax.shift_right_logical(values, jnp.full(values.shape, amount, jnp.int32))


def scramble(values):
    values = jnp.bitwise_xor(values, shift_down(values, 16))
    values = values * jnp.int32(-2048144789)
    values = jnp.bitwise_xor(values, shift_down(values, 13))
    values = values * jnp.int32(-1028477387)
    return jnp.bitwise_xor(values, shift_down(values, 16))


def head_word(seed_words, stream_offset, layer_index, head_ids):
    inner = scramble(head_ids + stream_offset[0])
    middle = scramble(layer_index[0] * jnp.int32(golden) + inner)
    return scramble(seed_words[0] + middle)


def rotation(positions):
    half_width = HD // 2
    exponent = jnp.arange(half_width, dtype=jnp.float32) * 2.0 / HD
    frequency = rope_theta ** (-exponent)
    angles = positions.astype(jnp.float32)[:, None] * frequency[None, :]
    return jnp.cos(angles), jnp.sin(angles)


def rotate(values, cosine, sine_part):
    half_width = HD // 2
    first_half = values[..., :half_width]
    second_half = values[..., half_width:]
    return jnp.concatenate(
        [
            first_half * cosine - second_half * sine_part,
            second_half * cosine + first_half * sine_part,
        ],
        axis=-1,
    )


def shards(activations, w_query, w_key, w_value, seed_words, stream_offset, layer_index):
    n_g = lax.axis_size("cg")
    n_t = lax.axis_size("ct")
    g = lax.axis_index("cg")
    t = lax.axis_index("ct")
    f = lax.axis_index("fsdp")
    tok = activations.shape[0]
    d_rows = w_query.shape[0]
    group_heads = HQ // KV
    local_heads = w_query.shape[1] // HD
    qcols = group_heads * HD
    rows = n_g * tok

    if lax.axis_size("fsdp") == 2:
        pieces = []
        halves = [activations]
        if n_g == 4:
            right = [(i, (i + 1) % n_g) for i in range(n_g)]
            left = [(i, (i - 1) % n_g) for i in range(n_g)]
            from_left = lax.ppermute(activations, "cg", right)
            from_right = lax.ppermute(activations, "cg", left)
            halves += [from_left, lax.ppermute(from_left, "cg", right), from_right]
        else:
            for shift in range(1, n_g):
                perm = [(i, (i + shift) % n_g) for i in range(n_g)]
                halves.append(lax.ppermute(activations, "cg", perm))
        for mine_half in halves:
            other_half = lax.ppermute(mine_half, "fsdp", [(0, 1), (1, 0)])
            pieces.append(
                jnp.where(
                    f == 0,
                    jnp.concatenate([mine_half, other_half], axis=1),
                    jnp.concatenate([other_half, mine_half], axis=1),
                )
            )
    else:
        own_half = [activations]
        for shift in range(1, n_g):
            perm = [(i, (i + shift) % n_g) for i in range(n_g)]
            own_half.append(lax.ppermute(activations, "cg", perm))
        grp_rows = lax.all_gather(jnp.concatenate(own_half, axis=0), "fsdp", axis=1, tiled=True)
        pieces = [grp_rows[i * tok : (i + 1) * tok] for i in range(n_g)]

    local_w = jnp.concatenate(
        [
            w_query.reshape(d_rows, n_g, qcols),
            w_key.reshape(d_rows, n_g, HD),
            w_value.reshape(d_rows, n_g, HD),
        ],
        axis=2,
    )
    received = [lax.dynamic_index_in_dim(local_w, g, 1, keepdims=False)]
    for shift in range(1, n_g):
        outgoing = lax.dynamic_index_in_dim(local_w, (g + shift) % n_g, 1, keepdims=False)
        perm = [(i, (i + shift) % n_g) for i in range(n_g)]
        received.append(lax.ppermute(outgoing, "cg", perm))
    by_shift = jnp.stack(received, axis=0)
    back = (g - jnp.arange(n_g, dtype=jnp.int32)) % n_g
    mine = jnp.take(by_shift, back, axis=0)
    every = lax.all_gather(mine, "ct", axis=0, tiled=False)
    every = every.transpose(1, 0, 2, 3).reshape(n_g * n_t * d_rows, qcols + 2 * HD)

    mixed = jnp.stack(
        [jnp.dot(piece, every, preferred_element_type=jnp.float32) for piece in pieces], axis=0
    )
    mixed = jnp.take(mixed, back, axis=0).reshape(rows, -1)
    chunk_of_row = n_t * (jnp.arange(rows, dtype=jnp.int32) // tok) + t
    positions = chunk_of_row * tok + jnp.arange(rows, dtype=jnp.int32) % tok
    cosine, sine_part = rotation(positions)
    queries = rotate(
        mixed[:, :qcols].reshape(rows, group_heads, HD), cosine[:, None, :], sine_part[:, None, :]
    ).astype(jnp.bfloat16)
    keys = rotate(mixed[:, qcols : qcols + HD], cosine, sine_part).astype(jnp.bfloat16)
    values = mixed[:, qcols + HD :].astype(jnp.bfloat16)

    pair = jnp.stack([keys, values], axis=1)
    pair = lax.all_gather(pair, "ct", axis=0, tiled=False)
    pair = pair.reshape(n_t, n_g, tok, 2, HD).transpose(1, 0, 2, 3, 4)
    pair = pair.reshape(n_g * n_t * tok, 2, HD)
    all_keys = pair[:, 0]
    all_values = pair[:, 1]

    head_global = f * local_heads + g * group_heads + jnp.arange(group_heads, dtype=jnp.int32)
    words = head_word(seed_words, stream_offset, layer_index, head_global)
    score_scale = HD ** (-0.5)
    pieces = []
    for chunk in range(n_g):
        span = n_t * (chunk + 1) * tok
        query_pos = (n_t * chunk + t) * tok + jnp.arange(tok, dtype=jnp.int32)
        key_pos = jnp.arange(span, dtype=jnp.int32)
        chunk_queries = queries[chunk * tok : (chunk + 1) * tok]
        scores = (
            jnp.einsum(
                "qhe,ke->hqk",
                chunk_queries,
                all_keys[:span],
                preferred_element_type=jnp.float32,
            )
            * score_scale
        )
        visible = key_pos[None, None, :] <= query_pos[None, :, None]
        highest = jnp.max(jnp.where(visible, scores, masked_score), axis=2, keepdims=True)
        weights = jnp.where(visible, jnp.exp(scores - highest), 0.0)
        summed = jnp.sum(weights, axis=2)
        row_words = scramble(jnp.bitwise_xor(words[:, None], query_pos[None, :]))
        mixed_bits = scramble(row_words[:, :, None] + (key_pos * jnp.int32(golden))[None, None, :])
        keep = shift_down(mixed_bits, 8) >= drop_level
        dropped = jnp.where(keep, weights, 0.0).astype(jnp.bfloat16)
        attended = jnp.einsum(
            "hqk,ke->hqe", dropped, all_values[:span], preferred_element_type=jnp.float32
        )
        result = (attended / (summed * (1.0 - drop_rate))[:, :, None]).astype(jnp.bfloat16)
        pieces.append(result.transpose(1, 0, 2).reshape(tok, qcols))
    out_rows = jnp.stack(pieces, axis=0)
    returned = lax.all_to_all(out_rows, "cg", split_axis=0, concat_axis=2, tiled=True)
    return returned.reshape(tok, n_g * qcols)


def solution(mesh):
    ctx = mesh.shape["ctx"]
    fsdp = mesh.shape["fsdp"]
    n_g = KV // fsdp
    n_t = ctx // n_g
    order = [mesh.axis_names.index("ctx"), mesh.axis_names.index("fsdp")]
    devices = np.transpose(mesh.devices, order).reshape(n_g, n_t, fsdp)
    grid = Mesh(devices, ("cg", "ct", "fsdp"))
    spec = P(("cg", "ct"), "fsdp")
    placed = (spec, spec, spec, spec, P(), P(), P())
    return jax.shard_map(shards, mesh=grid, in_specs=placed, out_specs=spec, check_vma=False)
```

```python
import jax
import jax.numpy as jnp
import numpy as np
from jax import lax
from jax.sharding import Mesh
from jax.sharding import PartitionSpec as P

HQ = 64
KV = 8
HD = 128


golden = -1640531535
drop_rate = 0.1
drop_level = 1677722
rope_theta = 500000.0
masked_score = -1e30


def shift_down(values, amount):
    return lax.shift_right_logical(values, jnp.full(values.shape, amount, jnp.int32))


def scramble(values):
    values = jnp.bitwise_xor(values, shift_down(values, 16))
    values = values * jnp.int32(-2048144789)
    values = jnp.bitwise_xor(values, shift_down(values, 13))
    values = values * jnp.int32(-1028477387)
    return jnp.bitwise_xor(values, shift_down(values, 16))


def head_word(seed_words, stream_offset, layer_index, head_ids):
    inner = scramble(head_ids + stream_offset[0])
    middle = scramble(layer_index[0] * jnp.int32(golden) + inner)
    return scramble(seed_words[0] + middle)


def rotation(positions):
    half_width = HD // 2
    exponent = jnp.arange(half_width, dtype=jnp.float32) * 2.0 / HD
    frequency = rope_theta ** (-exponent)
    angles = positions.astype(jnp.float32)[:, None] * frequency[None, :]
    return jnp.cos(angles), jnp.sin(angles)


def rotate(values, cosine, sine_part):
    half_width = HD // 2
    first_half = values[..., :half_width]
    second_half = values[..., half_width:]
    return jnp.concatenate(
        [
            first_half * cosine - second_half * sine_part,
            second_half * cosine + first_half * sine_part,
        ],
        axis=-1,
    )


def shards(activations, w_query, w_key, w_value, seed_words, stream_offset, layer_index):
    n_g = lax.axis_size("cg")
    n_t = lax.axis_size("ct")
    g = lax.axis_index("cg")
    t = lax.axis_index("ct")
    f = lax.axis_index("fsdp")
    tok = activations.shape[0]
    d_rows = w_query.shape[0]
    group_heads = HQ // KV
    local_heads = w_query.shape[1] // HD
    qcols = group_heads * HD
    rows = n_g * tok

    local_w = jnp.concatenate(
        [
            w_query.reshape(d_rows, n_g, qcols),
            w_key.reshape(d_rows, n_g, HD),
            w_value.reshape(d_rows, n_g, HD),
        ],
        axis=2,
    )
    if lax.axis_size("fsdp") == 2:
        own_other = lax.ppermute(activations, "fsdp", [(0, 1), (1, 0)])
        own_other, local_w = lax.optimization_barrier((own_other, local_w))
    received = [lax.dynamic_index_in_dim(local_w, g, 1, keepdims=False)]
    for shift in range(1, n_g):
        outgoing = lax.dynamic_index_in_dim(local_w, (g + shift) % n_g, 1, keepdims=False)
        perm = [(i, (i + shift) % n_g) for i in range(n_g)]
        received.append(lax.ppermute(outgoing, "cg", perm))
    by_shift = jnp.stack(received, axis=0)
    back = (g - jnp.arange(n_g, dtype=jnp.int32)) % n_g
    mine = jnp.take(by_shift, back, axis=0)
    if lax.axis_size("fsdp") == 2:
        pieces = []
        halves = [activations]
        if n_g == 4:
            right = [(i, (i + 1) % n_g) for i in range(n_g)]
            left = [(i, (i - 1) % n_g) for i in range(n_g)]
            from_left = lax.ppermute(activations, "cg", right)
            from_right = lax.ppermute(activations, "cg", left)
            halves += [from_left, lax.ppermute(from_left, "cg", right), from_right]
        else:
            for shift in range(1, n_g):
                perm = [(i, (i + shift) % n_g) for i in range(n_g)]
                halves.append(lax.ppermute(activations, "cg", perm))
        for index, mine_half in enumerate(halves):
            if index:
                other_half = lax.ppermute(mine_half, "fsdp", [(0, 1), (1, 0)])
            else:
                other_half = own_other
            pieces.append(
                jnp.where(
                    f == 0,
                    jnp.concatenate([mine_half, other_half], axis=1),
                    jnp.concatenate([other_half, mine_half], axis=1),
                )
            )
        grp_rows = jnp.concatenate(pieces, axis=0)
    else:
        own_half = [activations]
        for shift in range(1, n_g):
            perm = [(i, (i + shift) % n_g) for i in range(n_g)]
            own_half.append(lax.ppermute(activations, "cg", perm))
        grp_rows = lax.all_gather(jnp.concatenate(own_half, axis=0), "fsdp", axis=1, tiled=True)

    every = lax.all_gather(mine, "ct", axis=0, tiled=False)
    every = every.transpose(1, 0, 2, 3).reshape(n_g * n_t * d_rows, qcols + 2 * HD)

    mixed = jnp.dot(grp_rows, every, preferred_element_type=jnp.float32)
    mixed = jnp.take(mixed.reshape(n_g, tok, -1), back, axis=0).reshape(rows, -1)
    chunk_of_row = n_t * (jnp.arange(rows, dtype=jnp.int32) // tok) + t
    positions = chunk_of_row * tok + jnp.arange(rows, dtype=jnp.int32) % tok
    cosine, sine_part = rotation(positions)
    queries = rotate(
        mixed[:, :qcols].reshape(rows, group_heads, HD), cosine[:, None, :], sine_part[:, None, :]
    ).astype(jnp.bfloat16)
    keys = rotate(mixed[:, qcols : qcols + HD], cosine, sine_part).astype(jnp.bfloat16)
    values = mixed[:, qcols + HD :].astype(jnp.bfloat16)

    pair = jnp.stack([keys, values], axis=1)
    pair = lax.all_gather(pair, "ct", axis=0, tiled=False)
    pair = pair.reshape(n_t, n_g, tok, 2, HD).transpose(1, 0, 2, 3, 4)
    pair = pair.reshape(n_g * n_t * tok, 2, HD)
    all_keys = pair[:, 0]
    all_values = pair[:, 1]

    head_global = f * local_heads + g * group_heads + jnp.arange(group_heads, dtype=jnp.int32)
    words = head_word(seed_words, stream_offset, layer_index, head_global)
    score_scale = HD ** (-0.5)
    pieces = []
    for chunk in range(n_g):
        span = n_t * (chunk + 1) * tok
        query_pos = (n_t * chunk + t) * tok + jnp.arange(tok, dtype=jnp.int32)
        key_pos = jnp.arange(span, dtype=jnp.int32)
        chunk_queries = queries[chunk * tok : (chunk + 1) * tok]
        scores = (
            jnp.einsum(
                "qhe,ke->hqk",
                chunk_queries,
                all_keys[:span],
                preferred_element_type=jnp.float32,
            )
            * score_scale
        )
        visible = key_pos[None, None, :] <= query_pos[None, :, None]
        highest = jnp.max(jnp.where(visible, scores, masked_score), axis=2, keepdims=True)
        weights = jnp.where(visible, jnp.exp(scores - highest), 0.0)
        summed = jnp.sum(weights, axis=2)
        row_words = scramble(jnp.bitwise_xor(words[:, None], query_pos[None, :]))
        mixed_bits = scramble(row_words[:, :, None] + (key_pos * jnp.int32(golden))[None, None, :])
        keep = shift_down(mixed_bits, 8) >= drop_level
        dropped = jnp.where(keep, weights, 0.0).astype(jnp.bfloat16)
        attended = jnp.einsum(
            "hqk,ke->hqe", dropped, all_values[:span], preferred_element_type=jnp.float32
        )
        result = (attended / (summed * (1.0 - drop_rate))[:, :, None]).astype(jnp.bfloat16)
        pieces.append(result.transpose(1, 0, 2).reshape(tok, qcols))
    out_rows = jnp.stack(pieces, axis=0)
    returned = lax.all_to_all(out_rows, "cg", split_axis=0, concat_axis=2, tiled=True)
    return returned.reshape(tok, n_g * qcols)


def solution(mesh):
    ctx = mesh.shape["ctx"]
    fsdp = mesh.shape["fsdp"]
    n_g = KV // fsdp
    n_t = ctx // n_g
    order = [mesh.axis_names.index("ctx"), mesh.axis_names.index("fsdp")]
    devices = np.transpose(mesh.devices, order).reshape(n_g, n_t, fsdp)
    grid = Mesh(devices, ("cg", "ct", "fsdp"))
    spec = P(("cg", "ct"), "fsdp")
    placed = (spec, spec, spec, spec, P(), P(), P())
    return jax.shard_map(shards, mesh=grid, in_specs=placed, out_specs=spec, check_vma=False)
```

```python
import jax
import jax.numpy as jnp
import numpy as np
from jax import lax
from jax.sharding import Mesh
from jax.sharding import PartitionSpec as P

HQ = 64
KV = 8
HD = 128


golden = -1640531535
drop_rate = 0.1
drop_level = 1677722
rope_theta = 500000.0
masked_score = -1e30


def shift_down(values, amount):
    return lax.shift_right_logical(values, jnp.full(values.shape, amount, jnp.int32))


def scramble(values):
    values = jnp.bitwise_xor(values, shift_down(values, 16))
    values = values * jnp.int32(-2048144789)
    values = jnp.bitwise_xor(values, shift_down(values, 13))
    values = values * jnp.int32(-1028477387)
    return jnp.bitwise_xor(values, shift_down(values, 16))


def head_word(seed_words, stream_offset, layer_index, head_ids):
    inner = scramble(head_ids + stream_offset[0])
    middle = scramble(layer_index[0] * jnp.int32(golden) + inner)
    return scramble(seed_words[0] + middle)


def rotation(positions):
    half_width = HD // 2
    exponent = jnp.arange(half_width, dtype=jnp.float32) * 2.0 / HD
    frequency = rope_theta ** (-exponent)
    angles = positions.astype(jnp.float32)[:, None] * frequency[None, :]
    return jnp.cos(angles), jnp.sin(angles)


def rotate(values, cosine, sine_part):
    half_width = HD // 2
    first_half = values[..., :half_width]
    second_half = values[..., half_width:]
    return jnp.concatenate(
        [
            first_half * cosine - second_half * sine_part,
            second_half * cosine + first_half * sine_part,
        ],
        axis=-1,
    )


def shards(activations, w_query, w_key, w_value, seed_words, stream_offset, layer_index):
    n_g = lax.axis_size("cg")
    n_t = lax.axis_size("ct")
    g = lax.axis_index("cg")
    t = lax.axis_index("ct")
    f = lax.axis_index("fsdp")
    tok = activations.shape[0]
    d_rows = w_query.shape[0]
    group_heads = HQ // KV
    local_heads = w_query.shape[1] // HD
    qcols = group_heads * HD
    rows = n_g * tok

    local_w = jnp.concatenate(
        [
            w_query.reshape(d_rows, n_g, qcols),
            w_key.reshape(d_rows, n_g, HD),
            w_value.reshape(d_rows, n_g, HD),
        ],
        axis=2,
    )
    if lax.axis_size("fsdp") == 2:
        own_other = lax.ppermute(activations, "fsdp", [(0, 1), (1, 0)])
        own_other, local_w = lax.optimization_barrier((own_other, local_w))
    received = [lax.dynamic_index_in_dim(local_w, g, 1, keepdims=False)]
    for shift in range(1, n_g):
        outgoing = lax.dynamic_index_in_dim(local_w, (g + shift) % n_g, 1, keepdims=False)
        perm = [(i, (i + shift) % n_g) for i in range(n_g)]
        received.append(lax.ppermute(outgoing, "cg", perm))
    by_shift = jnp.stack(received, axis=0)
    back = (g - jnp.arange(n_g, dtype=jnp.int32)) % n_g
    mine = jnp.take(by_shift, back, axis=0)
    if lax.axis_size("fsdp") == 2:
        pieces = []
        halves = [activations]
        if n_g == 4:
            right = [(i, (i + 1) % n_g) for i in range(n_g)]
            left = [(i, (i - 1) % n_g) for i in range(n_g)]
            from_left = lax.ppermute(activations, "cg", right)
            from_right = lax.ppermute(activations, "cg", left)
            halves += [from_left, lax.ppermute(from_left, "cg", right), from_right]
        else:
            for shift in range(1, n_g):
                perm = [(i, (i + shift) % n_g) for i in range(n_g)]
                halves.append(lax.ppermute(activations, "cg", perm))
        others = [own_other] + [
            lax.ppermute(half, "fsdp", [(0, 1), (1, 0)]) for half in halves[1:]
        ]
        split_rows = (jnp.concatenate(halves, axis=0), jnp.concatenate(others, axis=0))
    else:
        own_half = [activations]
        for shift in range(1, n_g):
            perm = [(i, (i + shift) % n_g) for i in range(n_g)]
            own_half.append(lax.ppermute(activations, "cg", perm))
        grp_rows = lax.all_gather(jnp.concatenate(own_half, axis=0), "fsdp", axis=1, tiled=True)
        split_rows = None

    every = lax.all_gather(mine, "ct", axis=0, tiled=False)
    every = every.transpose(1, 0, 2, 3).reshape(n_g * n_t * d_rows, qcols + 2 * HD)

    if split_rows is None:
        mixed = jnp.dot(grp_rows, every, preferred_element_type=jnp.float32)
    else:
        halves_w = every.reshape(2, every.shape[0] // 2, every.shape[1])
        mine_w = lax.dynamic_index_in_dim(halves_w, f, 0, keepdims=False)
        other_w = lax.dynamic_index_in_dim(halves_w, 1 - f, 0, keepdims=False)
        mixed = jnp.dot(split_rows[0], mine_w, preferred_element_type=jnp.float32) + jnp.dot(
            split_rows[1], other_w, preferred_element_type=jnp.float32
        )
    mixed = jnp.take(mixed.reshape(n_g, tok, -1), back, axis=0).reshape(rows, -1)
    chunk_of_row = n_t * (jnp.arange(rows, dtype=jnp.int32) // tok) + t
    positions = chunk_of_row * tok + jnp.arange(rows, dtype=jnp.int32) % tok
    cosine, sine_part = rotation(positions)
    queries = rotate(
        mixed[:, :qcols].reshape(rows, group_heads, HD), cosine[:, None, :], sine_part[:, None, :]
    ).astype(jnp.bfloat16)
    keys = rotate(mixed[:, qcols : qcols + HD], cosine, sine_part).astype(jnp.bfloat16)
    values = mixed[:, qcols + HD :].astype(jnp.bfloat16)

    pair = jnp.stack([keys, values], axis=1)
    pair = lax.all_gather(pair, "ct", axis=0, tiled=False)
    pair = pair.reshape(n_t, n_g, tok, 2, HD).transpose(1, 0, 2, 3, 4)
    pair = pair.reshape(n_g * n_t * tok, 2, HD)
    all_keys = pair[:, 0]
    all_values = pair[:, 1]

    head_global = f * local_heads + g * group_heads + jnp.arange(group_heads, dtype=jnp.int32)
    words = head_word(seed_words, stream_offset, layer_index, head_global)
    score_scale = HD ** (-0.5)
    pieces = []
    for chunk in range(n_g):
        span = n_t * (chunk + 1) * tok
        query_pos = (n_t * chunk + t) * tok + jnp.arange(tok, dtype=jnp.int32)
        key_pos = jnp.arange(span, dtype=jnp.int32)
        chunk_queries = queries[chunk * tok : (chunk + 1) * tok]
        scores = (
            jnp.einsum(
                "qhe,ke->hqk",
                chunk_queries,
                all_keys[:span],
                preferred_element_type=jnp.float32,
            )
            * score_scale
        )
        visible = key_pos[None, None, :] <= query_pos[None, :, None]
        highest = jnp.max(jnp.where(visible, scores, masked_score), axis=2, keepdims=True)
        weights = jnp.where(visible, jnp.exp(scores - highest), 0.0)
        summed = jnp.sum(weights, axis=2)
        row_words = scramble(jnp.bitwise_xor(words[:, None], query_pos[None, :]))
        mixed_bits = scramble(row_words[:, :, None] + (key_pos * jnp.int32(golden))[None, None, :])
        keep = shift_down(mixed_bits, 8) >= drop_level
        dropped = jnp.where(keep, weights, 0.0).astype(jnp.bfloat16)
        attended = jnp.einsum(
            "hqk,ke->hqe", dropped, all_values[:span], preferred_element_type=jnp.float32
        )
        result = (attended / (summed * (1.0 - drop_rate))[:, :, None]).astype(jnp.bfloat16)
        pieces.append(result.transpose(1, 0, 2).reshape(tok, qcols))
    out_rows = jnp.stack(pieces, axis=0)
    returned = lax.all_to_all(out_rows, "cg", split_axis=0, concat_axis=2, tiled=True)
    return returned.reshape(tok, n_g * qcols)


def solution(mesh):
    ctx = mesh.shape["ctx"]
    fsdp = mesh.shape["fsdp"]
    n_g = KV // fsdp
    n_t = ctx // n_g
    order = [mesh.axis_names.index("ctx"), mesh.axis_names.index("fsdp")]
    devices = np.transpose(mesh.devices, order).reshape(n_g, n_t, fsdp)
    grid = Mesh(devices, ("cg", "ct", "fsdp"))
    spec = P(("cg", "ct"), "fsdp")
    placed = (spec, spec, spec, spec, P(), P(), P())
    return jax.shard_map(shards, mesh=grid, in_specs=placed, out_specs=spec, check_vma=False)
```

```python
import jax
import jax.numpy as jnp
import numpy as np
from jax import lax
from jax.sharding import Mesh
from jax.sharding import PartitionSpec as P

HQ = 64
KV = 8
HD = 128


golden = -1640531535
drop_rate = 0.1
drop_level = 1677722
rope_theta = 500000.0
masked_score = -1e30


def shift_down(values, amount):
    return lax.shift_right_logical(values, jnp.full(values.shape, amount, jnp.int32))


def scramble(values):
    values = jnp.bitwise_xor(values, shift_down(values, 16))
    values = values * jnp.int32(-2048144789)
    values = jnp.bitwise_xor(values, shift_down(values, 13))
    values = values * jnp.int32(-1028477387)
    return jnp.bitwise_xor(values, shift_down(values, 16))


def head_word(seed_words, stream_offset, layer_index, head_ids):
    inner = scramble(head_ids + stream_offset[0])
    middle = scramble(layer_index[0] * jnp.int32(golden) + inner)
    return scramble(seed_words[0] + middle)


def rotation(positions):
    half_width = HD // 2
    exponent = jnp.arange(half_width, dtype=jnp.float32) * 2.0 / HD
    frequency = rope_theta ** (-exponent)
    angles = positions.astype(jnp.float32)[:, None] * frequency[None, :]
    return jnp.cos(angles), jnp.sin(angles)


def rotate(values, cosine, sine_part):
    half_width = HD // 2
    first_half = values[..., :half_width]
    second_half = values[..., half_width:]
    return jnp.concatenate(
        [
            first_half * cosine - second_half * sine_part,
            second_half * cosine + first_half * sine_part,
        ],
        axis=-1,
    )


def shards(activations, w_query, w_key, w_value, seed_words, stream_offset, layer_index):
    n_g = lax.axis_size("cg")
    n_t = lax.axis_size("ct")
    g = lax.axis_index("cg")
    t = lax.axis_index("ct")
    f = lax.axis_index("fsdp")
    tok = activations.shape[0]
    d_rows = w_query.shape[0]
    group_heads = HQ // KV
    local_heads = w_query.shape[1] // HD
    qcols = group_heads * HD
    rows = n_g * tok

    local_w = jnp.concatenate(
        [
            w_query.reshape(d_rows, n_g, qcols),
            w_key.reshape(d_rows, n_g, HD),
            w_value.reshape(d_rows, n_g, HD),
        ],
        axis=2,
    )
    if lax.axis_size("fsdp") == 2:
        own_other = lax.ppermute(activations, "fsdp", [(0, 1), (1, 0)])
        own_other, local_w = lax.optimization_barrier((own_other, local_w))
    received = [lax.dynamic_index_in_dim(local_w, g, 1, keepdims=False)]
    for shift in range(1, n_g):
        outgoing = lax.dynamic_index_in_dim(local_w, (g + shift) % n_g, 1, keepdims=False)
        perm = [(i, (i + shift) % n_g) for i in range(n_g)]
        received.append(lax.ppermute(outgoing, "cg", perm))
    by_shift = jnp.stack(received, axis=0)
    back = (g - jnp.arange(n_g, dtype=jnp.int32)) % n_g
    if lax.axis_size("fsdp") == 2:
        pieces = []
        halves = [activations]
        if n_g == 4:
            right = [(i, (i + 1) % n_g) for i in range(n_g)]
            left = [(i, (i - 1) % n_g) for i in range(n_g)]
            from_left = lax.ppermute(activations, "cg", right)
            from_right = lax.ppermute(activations, "cg", left)
            halves += [from_left, lax.ppermute(from_left, "cg", right), from_right]
        else:
            for shift in range(1, n_g):
                perm = [(i, (i + shift) % n_g) for i in range(n_g)]
                halves.append(lax.ppermute(activations, "cg", perm))
        others = [own_other] + [
            lax.ppermute(half, "fsdp", [(0, 1), (1, 0)]) for half in halves[1:]
        ]
        split_rows = (jnp.concatenate(halves, axis=0), jnp.concatenate(others, axis=0))
    else:
        own_half = [activations]
        for shift in range(1, n_g):
            perm = [(i, (i + shift) % n_g) for i in range(n_g)]
            own_half.append(lax.ppermute(activations, "cg", perm))
        grp_rows = lax.all_gather(jnp.concatenate(own_half, axis=0), "fsdp", axis=1, tiled=True)
        split_rows = None

    every = lax.all_gather(by_shift, "ct", axis=0, tiled=False)
    every = jnp.take(every, back, axis=1).transpose(1, 0, 2, 3)
    every = every.reshape(n_g * n_t * d_rows, qcols + 2 * HD)

    if split_rows is None:
        mixed = jnp.dot(grp_rows, every, preferred_element_type=jnp.float32)
    else:
        halves_w = every.reshape(2, every.shape[0] // 2, every.shape[1])
        mine_w = lax.dynamic_index_in_dim(halves_w, f, 0, keepdims=False)
        other_w = lax.dynamic_index_in_dim(halves_w, 1 - f, 0, keepdims=False)
        mixed = jnp.dot(split_rows[0], mine_w, preferred_element_type=jnp.float32) + jnp.dot(
            split_rows[1], other_w, preferred_element_type=jnp.float32
        )
    shift_of_row = jnp.arange(rows, dtype=jnp.int32) // tok
    chunk_of_row = n_t * ((g - shift_of_row) % n_g) + t
    positions = chunk_of_row * tok + jnp.arange(rows, dtype=jnp.int32) % tok
    cosine, sine_part = rotation(positions)
    queries = rotate(
        mixed[:, :qcols].reshape(rows, group_heads, HD), cosine[:, None, :], sine_part[:, None, :]
    ).astype(jnp.bfloat16)
    keys = rotate(mixed[:, qcols : qcols + HD], cosine, sine_part).astype(jnp.bfloat16)
    values = mixed[:, qcols + HD :].astype(jnp.bfloat16)
    queries = jnp.take(queries.reshape(n_g, tok, group_heads, HD), back, axis=0)
    queries = queries.reshape(rows, group_heads, HD)
    keys = jnp.take(keys.reshape(n_g, tok, HD), back, axis=0).reshape(rows, HD)
    values = jnp.take(values.reshape(n_g, tok, HD), back, axis=0).reshape(rows, HD)

    pair = jnp.stack([keys, values], axis=1)
    pair = lax.all_gather(pair, "ct", axis=0, tiled=False)
    pair = pair.reshape(n_t, n_g, tok, 2, HD).transpose(1, 0, 2, 3, 4)
    pair = pair.reshape(n_g * n_t * tok, 2, HD)
    all_keys = pair[:, 0]
    all_values = pair[:, 1]

    head_global = f * local_heads + g * group_heads + jnp.arange(group_heads, dtype=jnp.int32)
    words = head_word(seed_words, stream_offset, layer_index, head_global)
    score_scale = HD ** (-0.5)
    pieces = []
    for chunk in range(n_g):
        span = n_t * (chunk + 1) * tok
        query_pos = (n_t * chunk + t) * tok + jnp.arange(tok, dtype=jnp.int32)
        key_pos = jnp.arange(span, dtype=jnp.int32)
        chunk_queries = queries[chunk * tok : (chunk + 1) * tok]
        scores = (
            jnp.einsum(
                "qhe,ke->hqk",
                chunk_queries,
                all_keys[:span],
                preferred_element_type=jnp.float32,
            )
            * score_scale
        )
        visible = key_pos[None, None, :] <= query_pos[None, :, None]
        highest = jnp.max(jnp.where(visible, scores, masked_score), axis=2, keepdims=True)
        weights = jnp.where(visible, jnp.exp(scores - highest), 0.0)
        summed = jnp.sum(weights, axis=2)
        row_words = scramble(jnp.bitwise_xor(words[:, None], query_pos[None, :]))
        mixed_bits = scramble(row_words[:, :, None] + (key_pos * jnp.int32(golden))[None, None, :])
        keep = shift_down(mixed_bits, 8) >= drop_level
        dropped = jnp.where(keep, weights, 0.0).astype(jnp.bfloat16)
        attended = jnp.einsum(
            "hqk,ke->hqe", dropped, all_values[:span], preferred_element_type=jnp.float32
        )
        result = (attended / (summed * (1.0 - drop_rate))[:, :, None]).astype(jnp.bfloat16)
        pieces.append(result.transpose(1, 0, 2).reshape(tok, qcols))
    out_rows = jnp.stack(pieces, axis=0)
    returned = lax.all_to_all(out_rows, "cg", split_axis=0, concat_axis=2, tiled=True)
    return returned.reshape(tok, n_g * qcols)


def solution(mesh):
    ctx = mesh.shape["ctx"]
    fsdp = mesh.shape["fsdp"]
    n_g = KV // fsdp
    n_t = ctx // n_g
    order = [mesh.axis_names.index("ctx"), mesh.axis_names.index("fsdp")]
    devices = np.transpose(mesh.devices, order).reshape(n_g, n_t, fsdp)
    grid = Mesh(devices, ("cg", "ct", "fsdp"))
    spec = P(("cg", "ct"), "fsdp")
    placed = (spec, spec, spec, spec, P(), P(), P())
    return jax.shard_map(shards, mesh=grid, in_specs=placed, out_specs=spec, check_vma=False)
```

```python
import jax
import jax.numpy as jnp
import numpy as np
from jax import lax
from jax.sharding import Mesh
from jax.sharding import PartitionSpec as P

HQ = 64
KV = 8
HD = 128


golden = -1640531535
drop_rate = 0.1
drop_level = 1677722
rope_theta = 500000.0
masked_score = -1e30


def shift_down(values, amount):
    return lax.shift_right_logical(values, jnp.full(values.shape, amount, jnp.int32))


def scramble(values):
    values = jnp.bitwise_xor(values, shift_down(values, 16))
    values = values * jnp.int32(-2048144789)
    values = jnp.bitwise_xor(values, shift_down(values, 13))
    values = values * jnp.int32(-1028477387)
    return jnp.bitwise_xor(values, shift_down(values, 16))


def head_word(seed_words, stream_offset, layer_index, head_ids):
    inner = scramble(head_ids + stream_offset[0])
    middle = scramble(layer_index[0] * jnp.int32(golden) + inner)
    return scramble(seed_words[0] + middle)


def rotation(positions):
    half_width = HD // 2
    exponent = jnp.arange(half_width, dtype=jnp.float32) * 2.0 / HD
    frequency = rope_theta ** (-exponent)
    angles = positions.astype(jnp.float32)[:, None] * frequency[None, :]
    return jnp.cos(angles), jnp.sin(angles)


def rotate(values, cosine, sine_part):
    half_width = HD // 2
    first_half = values[..., :half_width]
    second_half = values[..., half_width:]
    return jnp.concatenate(
        [
            first_half * cosine - second_half * sine_part,
            second_half * cosine + first_half * sine_part,
        ],
        axis=-1,
    )


def shards(activations, w_query, w_key, w_value, seed_words, stream_offset, layer_index):
    n_g = lax.axis_size("cg")
    n_t = lax.axis_size("ct")
    g = lax.axis_index("cg")
    t = lax.axis_index("ct")
    f = lax.axis_index("fsdp")
    tok = activations.shape[0]
    d_rows = w_query.shape[0]
    group_heads = HQ // KV
    local_heads = w_query.shape[1] // HD
    qcols = group_heads * HD
    rows = n_g * tok

    local_w = jnp.concatenate(
        [
            w_query.reshape(d_rows, n_g, qcols),
            w_key.reshape(d_rows, n_g, HD),
            w_value.reshape(d_rows, n_g, HD),
        ],
        axis=2,
    )
    if lax.axis_size("fsdp") == 2:
        own_other = lax.ppermute(activations, "fsdp", [(0, 1), (1, 0)])
        own_other, local_w = lax.optimization_barrier((own_other, local_w))
    received = [lax.dynamic_index_in_dim(local_w, g, 1, keepdims=False)]
    for shift in range(1, n_g):
        outgoing = lax.dynamic_index_in_dim(local_w, (g + shift) % n_g, 1, keepdims=False)
        perm = [(i, (i + shift) % n_g) for i in range(n_g)]
        received.append(lax.ppermute(outgoing, "cg", perm))
    by_shift = jnp.stack(received, axis=0)
    back = (g - jnp.arange(n_g, dtype=jnp.int32)) % n_g
    mine = jnp.take(by_shift, back, axis=0)
    if lax.axis_size("fsdp") == 2:
        pieces = []
        halves = [activations]
        if n_g == 4:
            right = [(i, (i + 1) % n_g) for i in range(n_g)]
            left = [(i, (i - 1) % n_g) for i in range(n_g)]
            from_left = lax.ppermute(activations, "cg", right)
            from_right = lax.ppermute(activations, "cg", left)
            halves += [from_left, lax.ppermute(from_left, "cg", right), from_right]
        else:
            for shift in range(1, n_g):
                perm = [(i, (i + shift) % n_g) for i in range(n_g)]
                halves.append(lax.ppermute(activations, "cg", perm))
        others = [own_other] + [
            lax.ppermute(half, "fsdp", [(0, 1), (1, 0)]) for half in halves[1:]
        ]
        split_rows = (jnp.concatenate(halves, axis=0), jnp.concatenate(others, axis=0))
    else:
        own_half = [activations]
        for shift in range(1, n_g):
            perm = [(i, (i + shift) % n_g) for i in range(n_g)]
            own_half.append(lax.ppermute(activations, "cg", perm))
        grp_rows = lax.all_gather(jnp.concatenate(own_half, axis=0), "fsdp", axis=1, tiled=True)
        split_rows = None

    every = lax.all_gather(mine, "ct", axis=0, tiled=False)
    every = every.transpose(1, 0, 2, 3).reshape(n_g * n_t * d_rows, qcols + 2 * HD)

    if split_rows is None:
        mixed = jnp.dot(grp_rows, every, preferred_element_type=jnp.float32)
    else:
        half = every.shape[0] // 2
        low_rows = jnp.where(f == 0, split_rows[0], split_rows[1])
        high_rows = jnp.where(f == 0, split_rows[1], split_rows[0])
        mixed = jnp.dot(low_rows, every[:half], preferred_element_type=jnp.float32) + jnp.dot(
            high_rows, every[half:], preferred_element_type=jnp.float32
        )
    shift_of_row = jnp.arange(rows, dtype=jnp.int32) // tok
    chunk_of_row = n_t * ((g - shift_of_row) % n_g) + t
    positions = chunk_of_row * tok + jnp.arange(rows, dtype=jnp.int32) % tok
    cosine, sine_part = rotation(positions)
    queries = rotate(
        mixed[:, :qcols].reshape(rows, group_heads, HD), cosine[:, None, :], sine_part[:, None, :]
    ).astype(jnp.bfloat16)
    keys = rotate(mixed[:, qcols : qcols + HD], cosine, sine_part).astype(jnp.bfloat16)
    values = mixed[:, qcols + HD :].astype(jnp.bfloat16)
    queries = jnp.take(queries.reshape(n_g, tok, group_heads, HD), back, axis=0)
    queries = queries.reshape(rows, group_heads, HD)
    keys = jnp.take(keys.reshape(n_g, tok, HD), back, axis=0).reshape(rows, HD)
    values = jnp.take(values.reshape(n_g, tok, HD), back, axis=0).reshape(rows, HD)

    pair = jnp.stack([keys, values], axis=1)
    pair = lax.all_gather(pair, "ct", axis=0, tiled=False)
    pair = pair.reshape(n_t, n_g, tok, 2, HD).transpose(1, 0, 2, 3, 4)
    pair = pair.reshape(n_g * n_t * tok, 2, HD)
    all_keys = pair[:, 0]
    all_values = pair[:, 1]

    head_global = f * local_heads + g * group_heads + jnp.arange(group_heads, dtype=jnp.int32)
    words = head_word(seed_words, stream_offset, layer_index, head_global)
    score_scale = HD ** (-0.5)
    pieces = []
    for chunk in range(n_g):
        span = n_t * (chunk + 1) * tok
        query_pos = (n_t * chunk + t) * tok + jnp.arange(tok, dtype=jnp.int32)
        key_pos = jnp.arange(span, dtype=jnp.int32)
        chunk_queries = queries[chunk * tok : (chunk + 1) * tok]
        scores = (
            jnp.einsum(
                "qhe,ke->hqk",
                chunk_queries,
                all_keys[:span],
                preferred_element_type=jnp.float32,
            )
            * score_scale
        )
        visible = key_pos[None, None, :] <= query_pos[None, :, None]
        highest = jnp.max(jnp.where(visible, scores, masked_score), axis=2, keepdims=True)
        weights = jnp.where(visible, jnp.exp(scores - highest), 0.0)
        summed = jnp.sum(weights, axis=2)
        row_words = scramble(jnp.bitwise_xor(words[:, None], query_pos[None, :]))
        mixed_bits = scramble(row_words[:, :, None] + (key_pos * jnp.int32(golden))[None, None, :])
        keep = shift_down(mixed_bits, 8) >= drop_level
        dropped = jnp.where(keep, weights, 0.0).astype(jnp.bfloat16)
        attended = jnp.einsum(
            "hqk,ke->hqe", dropped, all_values[:span], preferred_element_type=jnp.float32
        )
        result = (attended / (summed * (1.0 - drop_rate))[:, :, None]).astype(jnp.bfloat16)
        pieces.append(result.transpose(1, 0, 2).reshape(tok, qcols))
    out_rows = jnp.stack(pieces, axis=0)
    returned = lax.all_to_all(out_rows, "cg", split_axis=0, concat_axis=2, tiled=True)
    return returned.reshape(tok, n_g * qcols)


def solution(mesh):
    ctx = mesh.shape["ctx"]
    fsdp = mesh.shape["fsdp"]
    n_g = KV // fsdp
    n_t = ctx // n_g
    order = [mesh.axis_names.index("ctx"), mesh.axis_names.index("fsdp")]
    devices = np.transpose(mesh.devices, order).reshape(n_g, n_t, fsdp)
    grid = Mesh(devices, ("cg", "ct", "fsdp"))
    spec = P(("cg", "ct"), "fsdp")
    placed = (spec, spec, spec, spec, P(), P(), P())
    return jax.shard_map(shards, mesh=grid, in_specs=placed, out_specs=spec, check_vma=False)
```

```python
import jax
import jax.numpy as jnp
import numpy as np
from jax import lax
from jax.sharding import Mesh
from jax.sharding import PartitionSpec as P

HQ = 64
KV = 8
HD = 128


golden = -1640531535
drop_rate = 0.1
drop_level = 1677722
rope_theta = 500000.0
masked_score = -1e30


def shift_down(values, amount):
    return lax.shift_right_logical(values, jnp.full(values.shape, amount, jnp.int32))


def scramble(values):
    values = jnp.bitwise_xor(values, shift_down(values, 16))
    values = values * jnp.int32(-2048144789)
    values = jnp.bitwise_xor(values, shift_down(values, 13))
    values = values * jnp.int32(-1028477387)
    return jnp.bitwise_xor(values, shift_down(values, 16))


def head_word(seed_words, stream_offset, layer_index, head_ids):
    inner = scramble(head_ids + stream_offset[0])
    middle = scramble(layer_index[0] * jnp.int32(golden) + inner)
    return scramble(seed_words[0] + middle)


def rotation(positions):
    half_width = HD // 2
    exponent = jnp.arange(half_width, dtype=jnp.float32) * 2.0 / HD
    frequency = rope_theta ** (-exponent)
    angles = positions.astype(jnp.float32)[:, None] * frequency[None, :]
    return jnp.cos(angles), jnp.sin(angles)


def rotate(values, cosine, sine_part):
    half_width = HD // 2
    first_half = values[..., :half_width]
    second_half = values[..., half_width:]
    return jnp.concatenate(
        [
            first_half * cosine - second_half * sine_part,
            second_half * cosine + first_half * sine_part,
        ],
        axis=-1,
    )


def shards(activations, w_query, w_key, w_value, seed_words, stream_offset, layer_index):
    n_g = lax.axis_size("cg")
    n_t = lax.axis_size("ct")
    g = lax.axis_index("cg")
    t = lax.axis_index("ct")
    f = lax.axis_index("fsdp")
    tok = activations.shape[0]
    d_rows = w_query.shape[0]
    group_heads = HQ // KV
    local_heads = w_query.shape[1] // HD
    qcols = group_heads * HD
    rows = n_g * tok

    local_w = jnp.concatenate(
        [
            w_query.reshape(d_rows, n_g, qcols),
            w_key.reshape(d_rows, n_g, HD),
            w_value.reshape(d_rows, n_g, HD),
        ],
        axis=2,
    )
    if lax.axis_size("fsdp") == 2:
        own_other = lax.ppermute(activations, "fsdp", [(0, 1), (1, 0)])
        own_other, local_w = lax.optimization_barrier((own_other, local_w))
    received = [lax.dynamic_index_in_dim(local_w, g, 1, keepdims=False)]
    for shift in range(1, n_g):
        outgoing = lax.dynamic_index_in_dim(local_w, (g + shift) % n_g, 1, keepdims=False)
        perm = [(i, (i + shift) % n_g) for i in range(n_g)]
        received.append(lax.ppermute(outgoing, "cg", perm))
    by_shift = jnp.stack(received, axis=0)
    back = (g - jnp.arange(n_g, dtype=jnp.int32)) % n_g
    if lax.axis_size("fsdp") == 2:
        pieces = []
        halves = [activations]
        if n_g == 4:
            right = [(i, (i + 1) % n_g) for i in range(n_g)]
            left = [(i, (i - 1) % n_g) for i in range(n_g)]
            from_left = lax.ppermute(activations, "cg", right)
            from_right = lax.ppermute(activations, "cg", left)
            halves += [from_left, lax.ppermute(from_left, "cg", right), from_right]
        else:
            for shift in range(1, n_g):
                perm = [(i, (i + shift) % n_g) for i in range(n_g)]
                halves.append(lax.ppermute(activations, "cg", perm))
        others = [own_other] + [
            lax.ppermute(half, "fsdp", [(0, 1), (1, 0)]) for half in halves[1:]
        ]
        split_rows = (jnp.concatenate(halves, axis=0), jnp.concatenate(others, axis=0))
    else:
        own_half = [activations]
        for shift in range(1, n_g):
            perm = [(i, (i + shift) % n_g) for i in range(n_g)]
            own_half.append(lax.ppermute(activations, "cg", perm))
        grp_rows = lax.all_gather(jnp.concatenate(own_half, axis=0), "fsdp", axis=1, tiled=True)
        split_rows = None

    every = lax.all_gather(by_shift, "ct", axis=0, tiled=False)
    every = jnp.take(every.transpose(1, 0, 2, 3), back, axis=0)
    every = every.reshape(n_g * n_t * d_rows, qcols + 2 * HD)

    if split_rows is None:
        mixed = jnp.dot(grp_rows, every, preferred_element_type=jnp.float32)
    else:
        half = every.shape[0] // 2
        low_rows = jnp.where(f == 0, split_rows[0], split_rows[1])
        high_rows = jnp.where(f == 0, split_rows[1], split_rows[0])
        mixed = jnp.dot(low_rows, every[:half], preferred_element_type=jnp.float32) + jnp.dot(
            high_rows, every[half:], preferred_element_type=jnp.float32
        )
    shift_of_row = jnp.arange(rows, dtype=jnp.int32) // tok
    chunk_of_row = n_t * ((g - shift_of_row) % n_g) + t
    positions = chunk_of_row * tok + jnp.arange(rows, dtype=jnp.int32) % tok
    cosine, sine_part = rotation(positions)
    queries = rotate(
        mixed[:, :qcols].reshape(rows, group_heads, HD), cosine[:, None, :], sine_part[:, None, :]
    ).astype(jnp.bfloat16)
    keys = rotate(mixed[:, qcols : qcols + HD], cosine, sine_part).astype(jnp.bfloat16)
    values = mixed[:, qcols + HD :].astype(jnp.bfloat16)
    queries = jnp.take(queries.reshape(n_g, tok, group_heads, HD), back, axis=0)
    queries = queries.reshape(rows, group_heads, HD)
    keys = jnp.take(keys.reshape(n_g, tok, HD), back, axis=0).reshape(rows, HD)
    values = jnp.take(values.reshape(n_g, tok, HD), back, axis=0).reshape(rows, HD)

    pair = jnp.stack([keys, values], axis=1)
    pair = lax.all_gather(pair, "ct", axis=0, tiled=False)
    pair = pair.reshape(n_t, n_g, tok, 2, HD).transpose(1, 0, 2, 3, 4)
    pair = pair.reshape(n_g * n_t * tok, 2, HD)
    all_keys = pair[:, 0]
    all_values = pair[:, 1]

    head_global = f * local_heads + g * group_heads + jnp.arange(group_heads, dtype=jnp.int32)
    words = head_word(seed_words, stream_offset, layer_index, head_global)
    score_scale = HD ** (-0.5)
    pieces = []
    for chunk in range(n_g):
        span = n_t * (chunk + 1) * tok
        query_pos = (n_t * chunk + t) * tok + jnp.arange(tok, dtype=jnp.int32)
        key_pos = jnp.arange(span, dtype=jnp.int32)
        chunk_queries = queries[chunk * tok : (chunk + 1) * tok]
        scores = (
            jnp.einsum(
                "qhe,ke->hqk",
                chunk_queries,
                all_keys[:span],
                preferred_element_type=jnp.float32,
            )
            * score_scale
        )
        visible = key_pos[None, None, :] <= query_pos[None, :, None]
        highest = jnp.max(jnp.where(visible, scores, masked_score), axis=2, keepdims=True)
        weights = jnp.where(visible, jnp.exp(scores - highest), 0.0)
        summed = jnp.sum(weights, axis=2)
        row_words = scramble(jnp.bitwise_xor(words[:, None], query_pos[None, :]))
        mixed_bits = scramble(row_words[:, :, None] + (key_pos * jnp.int32(golden))[None, None, :])
        keep = shift_down(mixed_bits, 8) >= drop_level
        dropped = jnp.where(keep, weights, 0.0).astype(jnp.bfloat16)
        attended = jnp.einsum(
            "hqk,ke->hqe", dropped, all_values[:span], preferred_element_type=jnp.float32
        )
        result = (attended / (summed * (1.0 - drop_rate))[:, :, None]).astype(jnp.bfloat16)
        pieces.append(result.transpose(1, 0, 2).reshape(tok, qcols))
    out_rows = jnp.stack(pieces, axis=0)
    returned = lax.all_to_all(out_rows, "cg", split_axis=0, concat_axis=2, tiled=True)
    return returned.reshape(tok, n_g * qcols)


def solution(mesh):
    ctx = mesh.shape["ctx"]
    fsdp = mesh.shape["fsdp"]
    n_g = KV // fsdp
    n_t = ctx // n_g
    order = [mesh.axis_names.index("ctx"), mesh.axis_names.index("fsdp")]
    devices = np.transpose(mesh.devices, order).reshape(n_g, n_t, fsdp)
    grid = Mesh(devices, ("cg", "ct", "fsdp"))
    spec = P(("cg", "ct"), "fsdp")
    placed = (spec, spec, spec, spec, P(), P(), P())
    return jax.shard_map(shards, mesh=grid, in_specs=placed, out_specs=spec, check_vma=False)
```

```python
import jax
import jax.numpy as jnp
import numpy as np
from jax import lax
from jax.sharding import Mesh
from jax.sharding import PartitionSpec as P

HQ = 64
KV = 8
HD = 128


golden = -1640531535
drop_rate = 0.1
drop_level = 1677722
rope_theta = 500000.0
masked_score = -1e30


def shift_down(values, amount):
    return lax.shift_right_logical(values, jnp.full(values.shape, amount, jnp.int32))


def scramble(values):
    values = jnp.bitwise_xor(values, shift_down(values, 16))
    values = values * jnp.int32(-2048144789)
    values = jnp.bitwise_xor(values, shift_down(values, 13))
    values = values * jnp.int32(-1028477387)
    return jnp.bitwise_xor(values, shift_down(values, 16))


def head_word(seed_words, stream_offset, layer_index, head_ids):
    inner = scramble(head_ids + stream_offset[0])
    middle = scramble(layer_index[0] * jnp.int32(golden) + inner)
    return scramble(seed_words[0] + middle)


def rotation(positions):
    half_width = HD // 2
    exponent = jnp.arange(half_width, dtype=jnp.float32) * 2.0 / HD
    frequency = rope_theta ** (-exponent)
    angles = positions.astype(jnp.float32)[:, None] * frequency[None, :]
    return jnp.cos(angles), jnp.sin(angles)


def rotate(values, cosine, sine_part):
    half_width = HD // 2
    first_half = values[..., :half_width]
    second_half = values[..., half_width:]
    return jnp.concatenate(
        [
            first_half * cosine - second_half * sine_part,
            second_half * cosine + first_half * sine_part,
        ],
        axis=-1,
    )


def shards(activations, w_query, w_key, w_value, seed_words, stream_offset, layer_index):
    n_g = lax.axis_size("cg")
    n_t = lax.axis_size("ct")
    g = lax.axis_index("cg")
    t = lax.axis_index("ct")
    f = lax.axis_index("fsdp")
    tok = activations.shape[0]
    d_rows = w_query.shape[0]
    group_heads = HQ // KV
    local_heads = w_query.shape[1] // HD
    qcols = group_heads * HD
    rows = n_g * tok

    local_w = jnp.concatenate(
        [
            w_query.reshape(d_rows, n_g, qcols),
            w_key.reshape(d_rows, n_g, HD),
            w_value.reshape(d_rows, n_g, HD),
        ],
        axis=2,
    )
    if lax.axis_size("fsdp") == 2:
        own_other = lax.ppermute(activations, "fsdp", [(0, 1), (1, 0)])
        own_other, local_w = lax.optimization_barrier((own_other, local_w))
    received = [lax.dynamic_index_in_dim(local_w, g, 1, keepdims=False)]
    for shift in range(1, n_g):
        outgoing = lax.dynamic_index_in_dim(local_w, (g + shift) % n_g, 1, keepdims=False)
        perm = [(i, (i + shift) % n_g) for i in range(n_g)]
        received.append(lax.ppermute(outgoing, "cg", perm))
    by_shift = jnp.stack(received, axis=0)
    back = (g - jnp.arange(n_g, dtype=jnp.int32)) % n_g
    if lax.axis_size("fsdp") == 2:
        pieces = []
        halves = [activations]
        if n_g == 4:
            right = [(i, (i + 1) % n_g) for i in range(n_g)]
            left = [(i, (i - 1) % n_g) for i in range(n_g)]
            from_left = lax.ppermute(activations, "cg", right)
            from_right = lax.ppermute(activations, "cg", left)
            halves += [from_left, lax.ppermute(from_left, "cg", right), from_right]
        else:
            for shift in range(1, n_g):
                perm = [(i, (i + shift) % n_g) for i in range(n_g)]
                halves.append(lax.ppermute(activations, "cg", perm))
        others = [own_other] + [
            lax.ppermute(half, "fsdp", [(0, 1), (1, 0)]) for half in halves[1:]
        ]
        split_rows = (jnp.concatenate(halves, axis=0), jnp.concatenate(others, axis=0))
    else:
        own_half = [activations]
        for shift in range(1, n_g):
            perm = [(i, (i + shift) % n_g) for i in range(n_g)]
            own_half.append(lax.ppermute(activations, "cg", perm))
        grp_rows = lax.all_gather(jnp.concatenate(own_half, axis=0), "fsdp", axis=1, tiled=True)
        split_rows = None

    every = lax.all_gather(by_shift, "ct", axis=0, tiled=False)
    every = jnp.take(every, back, axis=1).transpose(1, 0, 2, 3)
    every = every.reshape(n_g * n_t * d_rows, qcols + 2 * HD)

    if split_rows is None:
        mixed = jnp.dot(grp_rows, every, preferred_element_type=jnp.float32)
    else:
        halves_w = every.reshape(2, every.shape[0] // 2, every.shape[1])
        mine_w = lax.dynamic_index_in_dim(halves_w, f, 0, keepdims=False)
        other_w = lax.dynamic_index_in_dim(halves_w, 1 - f, 0, keepdims=False)
        mixed = jnp.dot(split_rows[0], mine_w, preferred_element_type=jnp.float32) + jnp.dot(
            split_rows[1], other_w, preferred_element_type=jnp.float32
        )
    shift_of_row = jnp.arange(rows, dtype=jnp.int32) // tok
    chunk_of_row = n_t * ((g - shift_of_row) % n_g) + t
    positions = chunk_of_row * tok + jnp.arange(rows, dtype=jnp.int32) % tok
    cosine, sine_part = rotation(positions)
    queries = rotate(
        mixed[:, :qcols].reshape(rows, group_heads, HD), cosine[:, None, :], sine_part[:, None, :]
    ).astype(jnp.bfloat16)
    keys = rotate(mixed[:, qcols : qcols + HD], cosine, sine_part).astype(jnp.bfloat16)
    values = mixed[:, qcols + HD :].astype(jnp.bfloat16)
    queries = jnp.take(queries.reshape(n_g, tok, group_heads, HD), back, axis=0)
    queries = queries.reshape(rows, group_heads, HD)
    keys = jnp.take(keys.reshape(n_g, tok, HD), back, axis=0).reshape(rows, HD)
    values = jnp.take(values.reshape(n_g, tok, HD), back, axis=0).reshape(rows, HD)

    pair = jnp.stack([keys, values], axis=1)
    pair = lax.all_gather(pair, "ct", axis=0, tiled=False)
    pair = pair.reshape(n_t, n_g, tok, 2, HD).transpose(1, 0, 2, 3, 4)
    pair = pair.reshape(n_g * n_t * tok, 2, HD)
    all_keys = pair[:, 0]
    all_values = pair[:, 1]

    head_global = f * local_heads + g * group_heads + jnp.arange(group_heads, dtype=jnp.int32)
    words = head_word(seed_words, stream_offset, layer_index, head_global)
    score_scale = HD ** (-0.5)
    pieces = []
    for chunk in range(n_g):
        span = n_t * (chunk + 1) * tok
        query_pos = (n_t * chunk + t) * tok + jnp.arange(tok, dtype=jnp.int32)
        key_pos = jnp.arange(span, dtype=jnp.int32)
        chunk_queries = queries[chunk * tok : (chunk + 1) * tok]
        scores = (
            jnp.einsum(
                "qhe,ke->hqk",
                chunk_queries,
                all_keys[:span],
                preferred_element_type=jnp.float32,
            )
            * score_scale
        )
        visible = key_pos[None, None, :] <= query_pos[None, :, None]
        highest = jnp.max(jnp.where(visible, scores, masked_score), axis=2, keepdims=True)
        weights = jnp.where(visible, jnp.exp(scores - highest), 0.0)
        summed = jnp.sum(weights, axis=2)
        row_words = scramble(jnp.bitwise_xor(words[:, None], query_pos[None, :]))
        mixed_bits = scramble(row_words[:, :, None] + (key_pos * jnp.int32(golden))[None, None, :])
        keep = shift_down(mixed_bits, 8) >= drop_level
        dropped = jnp.where(keep, weights, 0.0).astype(jnp.bfloat16)
        attended = jnp.einsum(
            "hqk,ke->hqe", dropped, all_values[:span], preferred_element_type=jnp.float32
        )
        result = (attended / (summed * (1.0 - drop_rate))[:, :, None]).astype(jnp.bfloat16)
        pieces.append(result.transpose(1, 0, 2).reshape(tok, qcols))
    out_rows = jnp.stack(pieces, axis=0)
    arrived = [lax.dynamic_index_in_dim(out_rows, g, 0, keepdims=False)]
    for shift in range(1, n_g):
        outgoing = lax.dynamic_index_in_dim(out_rows, (g + shift) % n_g, 0, keepdims=False)
        perm = [(i, (i + shift) % n_g) for i in range(n_g)]
        arrived.append(lax.ppermute(outgoing, "cg", perm))
    returned = jnp.take(jnp.stack(arrived, axis=0), back, axis=0)
    return returned.transpose(1, 0, 2).reshape(tok, n_g * qcols)


def solution(mesh):
    ctx = mesh.shape["ctx"]
    fsdp = mesh.shape["fsdp"]
    n_g = KV // fsdp
    n_t = ctx // n_g
    order = [mesh.axis_names.index("ctx"), mesh.axis_names.index("fsdp")]
    devices = np.transpose(mesh.devices, order).reshape(n_g, n_t, fsdp)
    grid = Mesh(devices, ("cg", "ct", "fsdp"))
    spec = P(("cg", "ct"), "fsdp")
    placed = (spec, spec, spec, spec, P(), P(), P())
    return jax.shard_map(shards, mesh=grid, in_specs=placed, out_specs=spec, check_vma=False)
```

```python
import jax
import jax.numpy as jnp
import numpy as np
from jax import lax
from jax.sharding import Mesh
from jax.sharding import PartitionSpec as P

HQ = 64
KV = 8
HD = 128


golden = -1640531535
drop_rate = 0.1
drop_level = 1677722
rope_theta = 500000.0
masked_score = -1e30


def shift_down(values, amount):
    return lax.shift_right_logical(values, jnp.full(values.shape, amount, jnp.int32))


def scramble(values):
    values = jnp.bitwise_xor(values, shift_down(values, 16))
    values = values * jnp.int32(-2048144789)
    values = jnp.bitwise_xor(values, shift_down(values, 13))
    values = values * jnp.int32(-1028477387)
    return jnp.bitwise_xor(values, shift_down(values, 16))


def head_word(seed_words, stream_offset, layer_index, head_ids):
    inner = scramble(head_ids + stream_offset[0])
    middle = scramble(layer_index[0] * jnp.int32(golden) + inner)
    return scramble(seed_words[0] + middle)


def rotation(positions):
    half_width = HD // 2
    exponent = jnp.arange(half_width, dtype=jnp.float32) * 2.0 / HD
    frequency = rope_theta ** (-exponent)
    angles = positions.astype(jnp.float32)[:, None] * frequency[None, :]
    return jnp.cos(angles), jnp.sin(angles)


def rotate(values, cosine, sine_part):
    half_width = HD // 2
    first_half = values[..., :half_width]
    second_half = values[..., half_width:]
    return jnp.concatenate(
        [
            first_half * cosine - second_half * sine_part,
            second_half * cosine + first_half * sine_part,
        ],
        axis=-1,
    )


def shards(activations, w_query, w_key, w_value, seed_words, stream_offset, layer_index):
    n_g = lax.axis_size("cg")
    n_t = lax.axis_size("ct")
    g = lax.axis_index("cg")
    t = lax.axis_index("ct")
    f = lax.axis_index("fsdp")
    tok = activations.shape[0]
    d_rows = w_query.shape[0]
    group_heads = HQ // KV
    local_heads = w_query.shape[1] // HD
    qcols = group_heads * HD
    rows = n_g * tok

    local_w = jnp.concatenate(
        [
            w_query.reshape(d_rows, n_g, qcols),
            w_key.reshape(d_rows, n_g, HD),
            w_value.reshape(d_rows, n_g, HD),
        ],
        axis=2,
    )
    if lax.axis_size("fsdp") == 2:
        own_other = lax.ppermute(activations, "fsdp", [(0, 1), (1, 0)])
        own_other, local_w = lax.optimization_barrier((own_other, local_w))
    received = [lax.dynamic_index_in_dim(local_w, g, 1, keepdims=False)]
    for shift in range(1, n_g):
        outgoing = lax.dynamic_index_in_dim(local_w, (g + shift) % n_g, 1, keepdims=False)
        perm = [(i, (i + shift) % n_g) for i in range(n_g)]
        received.append(lax.ppermute(outgoing, "cg", perm))
    by_shift = jnp.stack(received, axis=0)
    back = (g - jnp.arange(n_g, dtype=jnp.int32)) % n_g
    if lax.axis_size("fsdp") == 2:
        pieces = []
        halves = [activations]
        if n_g == 4:
            right = [(i, (i + 1) % n_g) for i in range(n_g)]
            left = [(i, (i - 1) % n_g) for i in range(n_g)]
            from_left = lax.ppermute(activations, "cg", right)
            from_right = lax.ppermute(activations, "cg", left)
            halves += [from_left, lax.ppermute(from_left, "cg", right), from_right]
        else:
            for shift in range(1, n_g):
                perm = [(i, (i + shift) % n_g) for i in range(n_g)]
                halves.append(lax.ppermute(activations, "cg", perm))
        others = [own_other] + [
            lax.ppermute(half, "fsdp", [(0, 1), (1, 0)]) for half in halves[1:]
        ]
        split_rows = (jnp.concatenate(halves, axis=0), jnp.concatenate(others, axis=0))
    else:
        own_half = [activations]
        for shift in range(1, n_g):
            perm = [(i, (i + shift) % n_g) for i in range(n_g)]
            own_half.append(lax.ppermute(activations, "cg", perm))
        grp_rows = lax.all_gather(jnp.concatenate(own_half, axis=0), "fsdp", axis=1, tiled=True)
        split_rows = None

    every = lax.all_gather(by_shift, "ct", axis=0, tiled=False)
    slots = []
    for slot in range(n_g):
        chosen = every[:, 0]
        for shift in range(1, n_g):
            chosen = jnp.where(back[slot] == shift, every[:, shift], chosen)
        slots.append(chosen)
    every = jnp.stack(slots, axis=0)
    every = every.reshape(n_g * n_t * d_rows, qcols + 2 * HD)

    if split_rows is None:
        mixed = jnp.dot(grp_rows, every, preferred_element_type=jnp.float32)
    else:
        halves_w = every.reshape(2, every.shape[0] // 2, every.shape[1])
        mine_w = lax.dynamic_index_in_dim(halves_w, f, 0, keepdims=False)
        other_w = lax.dynamic_index_in_dim(halves_w, 1 - f, 0, keepdims=False)
        mixed = jnp.dot(split_rows[0], mine_w, preferred_element_type=jnp.float32) + jnp.dot(
            split_rows[1], other_w, preferred_element_type=jnp.float32
        )
    shift_of_row = jnp.arange(rows, dtype=jnp.int32) // tok
    chunk_of_row = n_t * ((g - shift_of_row) % n_g) + t
    positions = chunk_of_row * tok + jnp.arange(rows, dtype=jnp.int32) % tok
    cosine, sine_part = rotation(positions)
    queries = rotate(
        mixed[:, :qcols].reshape(rows, group_heads, HD), cosine[:, None, :], sine_part[:, None, :]
    ).astype(jnp.bfloat16)
    keys = rotate(mixed[:, qcols : qcols + HD], cosine, sine_part).astype(jnp.bfloat16)
    values = mixed[:, qcols + HD :].astype(jnp.bfloat16)
    queries = jnp.take(queries.reshape(n_g, tok, group_heads, HD), back, axis=0)
    queries = queries.reshape(rows, group_heads, HD)
    keys = jnp.take(keys.reshape(n_g, tok, HD), back, axis=0).reshape(rows, HD)
    values = jnp.take(values.reshape(n_g, tok, HD), back, axis=0).reshape(rows, HD)

    pair = jnp.stack([keys, values], axis=1)
    pair = lax.all_gather(pair, "ct", axis=0, tiled=False)
    pair = pair.reshape(n_t, n_g, tok, 2, HD).transpose(1, 0, 2, 3, 4)
    pair = pair.reshape(n_g * n_t * tok, 2, HD)
    all_keys = pair[:, 0]
    all_values = pair[:, 1]

    head_global = f * local_heads + g * group_heads + jnp.arange(group_heads, dtype=jnp.int32)
    words = head_word(seed_words, stream_offset, layer_index, head_global)
    score_scale = HD ** (-0.5)
    pieces = []
    for chunk in range(n_g):
        span = n_t * (chunk + 1) * tok
        query_pos = (n_t * chunk + t) * tok + jnp.arange(tok, dtype=jnp.int32)
        key_pos = jnp.arange(span, dtype=jnp.int32)
        chunk_queries = queries[chunk * tok : (chunk + 1) * tok]
        scores = (
            jnp.einsum(
                "qhe,ke->hqk",
                chunk_queries,
                all_keys[:span],
                preferred_element_type=jnp.float32,
            )
            * score_scale
        )
        visible = key_pos[None, None, :] <= query_pos[None, :, None]
        highest = jnp.max(jnp.where(visible, scores, masked_score), axis=2, keepdims=True)
        weights = jnp.where(visible, jnp.exp(scores - highest), 0.0)
        summed = jnp.sum(weights, axis=2)
        row_words = scramble(jnp.bitwise_xor(words[:, None], query_pos[None, :]))
        mixed_bits = scramble(row_words[:, :, None] + (key_pos * jnp.int32(golden))[None, None, :])
        keep = shift_down(mixed_bits, 8) >= drop_level
        dropped = jnp.where(keep, weights, 0.0).astype(jnp.bfloat16)
        attended = jnp.einsum(
            "hqk,ke->hqe", dropped, all_values[:span], preferred_element_type=jnp.float32
        )
        result = (attended / (summed * (1.0 - drop_rate))[:, :, None]).astype(jnp.bfloat16)
        pieces.append(result.transpose(1, 0, 2).reshape(tok, qcols))
    out_rows = jnp.stack(pieces, axis=0)
    returned = lax.all_to_all(out_rows, "cg", split_axis=0, concat_axis=2, tiled=True)
    return returned.reshape(tok, n_g * qcols)


def solution(mesh):
    ctx = mesh.shape["ctx"]
    fsdp = mesh.shape["fsdp"]
    n_g = KV // fsdp
    n_t = ctx // n_g
    order = [mesh.axis_names.index("ctx"), mesh.axis_names.index("fsdp")]
    devices = np.transpose(mesh.devices, order).reshape(n_g, n_t, fsdp)
    grid = Mesh(devices, ("cg", "ct", "fsdp"))
    spec = P(("cg", "ct"), "fsdp")
    placed = (spec, spec, spec, spec, P(), P(), P())
    return jax.shard_map(shards, mesh=grid, in_specs=placed, out_specs=spec, check_vma=False)
```
